128 devices in a mesh: dp: 4 (over z_hi, core), ctx: 32 (over x, y, z_lo).
Axes of the slice: x: 4, y: 4, z: 4 (z_hi: 2, z_lo: 2; z = z_hi * 2 + z_lo), core: 2. Of those that a mesh axis runs over, the one named last changes fastest.
Arguments:
- hidden: bfloat16 [4, 8192, 8192], P('dp', 'ctx')
- norm_gain: bfloat16 [8192], replicated, may hold values from 0.5 to 2
- queries: bfloat16 [4, 8192, 4096], P('dp', 'ctx')
- key_weight: bfloat16 [8192, 512], P('dp'), may hold values from -0.0625 to 0.0625
- value_weight: bfloat16 [8192, 512], P('dp'), may hold values from -0.0625 to 0.0625
- block_lists: int32 [4, 32, 64, 12], P('dp', 'ctx'), may hold values from 0 to 63, as said below
- block_counts: int32 [4, 32, 64], P('dp', 'ctx'), may hold values from 1 to 12, as said below
Outputs:
- attended: bfloat16 [4, 8192, 4096], P('dp', 'ctx')
The draws below stay inside these ranges and needn't reach their ends.
Inputs may be any that keep to these rules, and one draw needn't show every extreme that they name: `block_lists`: for each spreadsheet, head and query block i, the first block_counts entries are distinct key blocks: the first is i, each later one is smaller than the one before (the blocks of i's ancestors in that head's header tree, nearest first); entries past the count equal i and are to be ignored. `block_counts`: every spreadsheet has a query block with 12 listed blocks; the counts differ much from head to head.
All inputs are finite; a program needn't handle non-finite values.
Results may differ from the reference program's by a relative error of at most 0.0078.
Values may be sent and summed in bfloat16 or wider, within the bound.
No kernel may reach another device: no remote copies, remote signals or barrier semaphores. Data moves between devices by JAX's collectives and lax.ppermute only.
A program may use at most 128 MiB of HBM per device.

```python
import math
import jax
import jax.numpy as jnp
from jax import lax

D = 8192
QH = 32
KVH = 4
HD = 128
BLK = 128
MAXB = 12
BATCH = 4
SEQ = 8192
NB = 64


def draw_hidden(key, part):
    first, second, third = jax.random.split(key, 3)
    row_scale = jnp.exp(jax.random.uniform(second, (BATCH, SEQ, 1), minval=0.0, maxval=math.log(10.0)))
    col_scale = jnp.exp(jax.random.uniform(third, (D,), minval=0.0, maxval=math.log(10.0)))
    base = jax.random.normal(first, (BATCH, SEQ, D))
    return (base * row_scale * col_scale).astype(jnp.bfloat16)


def draw_queries(key, part):
    first = jax.random.fold_in(key, 0)
    base = jax.random.normal(first, (BATCH, SEQ, QH * HD))
    return base.astype(jnp.bfloat16)


def ancestry(key):
    key_thr, key_coin, key_far, key_head, key_start = jax.random.split(key, 5)
    blocks = jnp.arange(NB, dtype=jnp.int32)
    threshold = jax.random.randint(key_thr, (BATCH, QH, 1), 1, 10)
    coins = jax.random.randint(key_coin, (BATCH, QH, NB), 0, 10)
    far_parent = jax.random.randint(key_far, (BATCH, QH, NB), 0, jnp.maximum(blocks, 1))
    parent = jnp.maximum(jnp.where(coins < threshold, blocks - 1, far_parent), 0)
    forced_head = jax.random.randint(key_head, (BATCH, 1, 1), 0, QH)
    chain_end = jax.random.randint(key_start, (BATCH, 1, 1), MAXB - 1, NB)
    in_chain = (jnp.arange(QH)[None, :, None] == forced_head) & (blocks > chain_end - MAXB + 1) & (blocks <= chain_end)
    parent = jnp.where(in_chain, blocks - 1, parent).astype(jnp.int32)
    current = jnp.broadcast_to(blocks, (BATCH, QH, NB))
    entries = [current]
    alive = current != 0
    counted = jnp.ones((BATCH, QH, NB), jnp.int32)
    for step_index in range(MAXB - 1):
        following = jnp.take_along_axis(parent, current, axis=2)
        entries.append(jnp.where(alive, following, blocks))
        counted = counted + alive.astype(jnp.int32)
        alive = alive & (following != 0)
        current = following
    return (jnp.stack(entries, axis=-1).astype(jnp.int32), counted.astype(jnp.int32))


def draw_block_lists(key, part):
    return ancestry(jax.random.fold_in(key, 11))[0]


def draw_block_counts(key, part):
    return ancestry(jax.random.fold_in(key, 11))[1]


def shard_levels(own_key, extent, shards, least, largest):
    gain, own = 1.0, jax.random.fold_in(own_key, 6)
    for axis_at, parts in shards:
        heights = jnp.exp(jax.random.uniform(jax.random.fold_in(own, axis_at), (parts,), jnp.float32, least / len(shards), largest / len(shards)))
        gain = gain * jnp.repeat(heights, extent[axis_at] // parts).reshape([-1 if axis == axis_at else 1 for axis in range(len(extent))])
    return gain


def bell_draw(own_key, shape, scale, most, cuts=(), kind=jnp.bfloat16):
    gain = shard_levels(own_key, shape, cuts, -0.22, 0.18) if cuts else 1.0
    values = jax.random.normal(own_key, shape, jnp.float32) * scale * gain
    return jnp.minimum(jnp.maximum(values, -most), most).astype(kind)


def setup_inputs(seed: int = 0) -> dict:
    splits = jax.random.split(jax.random.key(seed), 8)
    hidden = draw_hidden(jax.random.fold_in(splits[7], 71), 0)
    norm_gain = jnp.clip(jnp.exp(jax.random.uniform(splits[1], (D,), jnp.float32, math.log(0.5), math.log(2.0))), 0.5, 2.0).astype(jnp.bfloat16)
    queries = draw_queries(jax.random.fold_in(splits[7], 71), 0)
    key_weight = bell_draw(splits[3], (D, KVH * HD), D ** -0.5, 0.0625, ((0, 4),))
    value_weight = bell_draw(splits[4], (D, KVH * HD), D ** -0.5, 0.0625, ((0, 4),))
    block_lists = draw_block_lists(jax.random.fold_in(splits[7], 71), 0)
    block_counts = draw_block_counts(jax.random.fold_in(splits[7], 71), 0)
    return dict(hidden=hidden, norm_gain=norm_gain, queries=queries, key_weight=key_weight, value_weight=value_weight, block_lists=block_lists, block_counts=block_counts)


def attend_head(bundle):
    query_head, key_head, value_head, lists_one, counts_one = bundle
    score_scale = HD ** (-0.5)
    query_tiles = query_head.reshape(NB, BLK, HD).astype(jnp.float32)
    key_tiles = jnp.take(key_head.reshape(NB, BLK, HD), lists_one, axis=0).astype(jnp.float32)
    value_tiles = jnp.take(value_head.reshape(NB, BLK, HD), lists_one, axis=0).astype(jnp.float32)
    scores = jnp.einsum('ntd,nskd->ntsk', query_tiles, key_tiles) * score_scale
    slot_ids = jnp.arange(MAXB)
    live_slots = slot_ids[None, :] < counts_one[:, None]
    causal = (slot_ids[None, :, None] > 0) | (jnp.arange(BLK)[None, None, :] <= jnp.arange(BLK)[:, None, None])
    allowed = live_slots[:, None, :, None] & causal[None]
    masked = jnp.where(allowed, scores, -jnp.inf)
    row_peak = lax.optimization_barrier(jnp.max(masked, axis=(2, 3), keepdims=True))
    exponent = jnp.exp(masked - row_peak)
    denominator = lax.optimization_barrier(jnp.sum(exponent, axis=(2, 3)))
    rounded = lax.optimization_barrier(exponent.astype(jnp.bfloat16)).astype(jnp.float32)
    weighted = jnp.einsum('ntsk,nskd->ntd', rounded, value_tiles)
    return (weighted / denominator[..., None]).astype(jnp.bfloat16).reshape(SEQ, HD)

def reference(hidden, norm_gain, queries, key_weight, value_weight, block_lists, block_counts):
    upcast = hidden.astype(jnp.float32)
    mean_square = lax.optimization_barrier(jnp.mean(upcast * upcast, axis=-1, keepdims=True))
    normed = (upcast * lax.rsqrt(mean_square + 1e-05) * norm_gain.astype(jnp.float32)).astype(jnp.bfloat16)
    flat_rows = normed.reshape(BATCH * SEQ, D)
    keys_all = jnp.dot(flat_rows, key_weight, preferred_element_type=jnp.float32).astype(jnp.bfloat16)
    values_all = jnp.dot(flat_rows, value_weight, preferred_element_type=jnp.float32).astype(jnp.bfloat16)
    group_size = QH // KVH
    key_heads = jnp.repeat(jnp.transpose(keys_all.reshape(BATCH, SEQ, KVH, HD), (0, 2, 1, 3)), group_size, axis=1).reshape(BATCH * QH, SEQ, HD)
    value_heads = jnp.repeat(jnp.transpose(values_all.reshape(BATCH, SEQ, KVH, HD), (0, 2, 1, 3)), group_size, axis=1).reshape(BATCH * QH, SEQ, HD)
    query_heads = jnp.transpose(queries.reshape(BATCH, SEQ, QH, HD), (0, 2, 1, 3)).reshape(BATCH * QH, SEQ, HD)
    lists_flat = block_lists.reshape(BATCH * QH, NB, MAXB)
    counts_flat = block_counts.reshape(BATCH * QH, NB)
    results = lax.map(attend_head, (query_heads, key_heads, value_heads, lists_flat, counts_flat))
    return jnp.transpose(results.reshape(BATCH, QH, SEQ, HD), (0, 2, 1, 3)).reshape(BATCH, SEQ, QH * HD)
```

```python
import jax
import jax.numpy as jnp
from jax import lax
from jax.experimental import pallas as pl
from jax.experimental.pallas import tpu as pltpu
from jax.sharding import PartitionSpec as P

KVH = 4
HD = 128
BLK = 128
MAXB = 12


def attend_kernel(lists_ref, counts_ref, q_ref, k_ref, v_ref, o_ref):
    block = pl.program_id(0)
    query = q_ref[...]
    count = counts_ref[block]
    score_scale = HD ** (-0.5)
    rows = lax.broadcasted_iota(jnp.int32, (BLK, BLK), 0)
    cols = lax.broadcasted_iota(jnp.int32, (BLK, BLK), 1)
    masked = []
    for slot in range(MAXB):
        start = pl.multiple_of(lists_ref[block * MAXB + slot] * BLK, BLK)
        key_tile = k_ref[pl.ds(start, BLK), :]
        scores = (
            lax.dot_general(
                query, key_tile, (((1,), (1,)), ((), ())), preferred_element_type=jnp.float32
            )
            * score_scale
        )
        allowed = slot < count
        if slot == 0:
            allowed = jnp.logical_and(allowed, cols <= rows)
        masked.append(jnp.where(allowed, scores, -jnp.inf))
    peak = masked[0]
    for scores in masked[1:]:
        peak = jnp.maximum(peak, scores)
    row_peak = jnp.max(peak, axis=1, keepdims=True)
    denominator = jnp.zeros((BLK, 1), jnp.float32)
    weighted = jnp.zeros((BLK, HD), jnp.float32)
    for slot in range(MAXB):
        start = pl.multiple_of(lists_ref[block * MAXB + slot] * BLK, BLK)
        value_tile = v_ref[pl.ds(start, BLK), :]
        exponent = jnp.exp(masked[slot] - row_peak)
        denominator = denominator + jnp.sum(exponent, axis=1, keepdims=True)
        weighted = weighted + jnp.dot(
            exponent.astype(jnp.bfloat16), value_tile, preferred_element_type=jnp.float32
        )
    o_ref[...] = (weighted / denominator).astype(o_ref.dtype)


def attend(lists_flat, counts, head_queries, kv_rows):
    sequence_rows = head_queries.shape[0]
    block_total = sequence_rows // BLK
    return pl.pallas_call(
        attend_kernel,
        out_shape=jax.ShapeDtypeStruct((sequence_rows, HD), jnp.bfloat16),
        grid_spec=pltpu.PrefetchScalarGridSpec(
            num_scalar_prefetch=2,
            grid=(block_total,),
            in_specs=[
                pl.BlockSpec((BLK, HD), lambda i, lists, counts: (i, 0)),
                pl.BlockSpec((sequence_rows, HD), lambda i, lists, counts: (0, 0)),
                pl.BlockSpec((sequence_rows, HD), lambda i, lists, counts: (0, 1)),
            ],
            out_specs=pl.BlockSpec((BLK, HD), lambda i, lists, counts: (i, 0)),
        ),
        compiler_params=pltpu.CompilerParams(dimension_semantics=("arbitrary",)),
    )(lists_flat, counts, head_queries, kv_rows, kv_rows)


def on_device(hidden, norm_gain, queries, key_weight, value_weight, block_lists, block_counts):
    upcast = hidden[0].astype(jnp.float32)
    mean_square = jnp.mean(upcast * upcast, axis=-1, keepdims=True)
    normed = (upcast * lax.rsqrt(mean_square + 1e-05) * norm_gain.astype(jnp.float32)).astype(
        jnp.bfloat16
    )
    local_rows = normed.shape[0]
    key_part = jnp.dot(
        normed,
        lax.all_gather(key_weight, "dp", axis=0, tiled=True),
        preferred_element_type=jnp.float32,
    )
    value_part = jnp.dot(
        normed,
        lax.all_gather(value_weight, "dp", axis=0, tiled=True),
        preferred_element_type=jnp.float32,
    )
    paired = jnp.stack([key_part, value_part], axis=1).astype(jnp.bfloat16)
    ctx_size = lax.axis_size("ctx")
    copies_per_head = ctx_size // KVH
    widened = jnp.broadcast_to(
        paired.reshape(local_rows, 2, KVH, 1, HD), (local_rows, 2, KVH, copies_per_head, HD)
    )
    widened = widened.reshape(local_rows, 2, ctx_size, HD)
    head_pair = lax.all_to_all(widened, "ctx", split_axis=2, concat_axis=0, tiled=True)
    head_queries = lax.all_to_all(queries[0], "ctx", split_axis=1, concat_axis=0, tiled=True)
    sequence_rows = head_queries.shape[0]
    kv_rows = head_pair.reshape(sequence_rows, 2 * HD)
    lists_flat = block_lists[0, 0].reshape(-1)
    counts = block_counts[0, 0]
    attended_head = attend(lists_flat, counts, head_queries, kv_rows)
    restored = lax.all_to_all(attended_head, "ctx", split_axis=0, concat_axis=1, tiled=True)
    return restored[None]


def solution(mesh):
    return jax.shard_map(
        on_device,
        mesh=mesh,
        in_specs=(
            P("dp", "ctx", None),
            P(),
            P("dp", "ctx", None),
            P("dp", None),
            P("dp", None),
            P("dp", "ctx", None, None),
            P("dp", "ctx", None),
        ),
        out_specs=P("dp", "ctx", None),
        check_vma=False,
    )
```

```python
import jax
import jax.numpy as jnp
from jax import lax
from jax.experimental import pallas as pl
from jax.experimental.pallas import tpu as pltpu
from jax.sharding import PartitionSpec as P

KVH = 4
HD = 128
BLK = 128
MAXB = 12


def attend_kernel(lists_ref, counts_ref, q_ref, k_ref, v_ref, o_ref):
    block = pl.program_id(0)
    query = q_ref[...]
    count = counts_ref[block]
    score_scale = HD ** (-0.5)
    rows = lax.broadcasted_iota(jnp.int32, (BLK, BLK), 0)
    cols = lax.broadcasted_iota(jnp.int32, (BLK, BLK), 1)
    masked = []
    for slot in range(MAXB):
        start = pl.multiple_of(lists_ref[block * MAXB + slot] * BLK, BLK)
        key_tile = k_ref[pl.ds(start, BLK), :]
        scores = (
            lax.dot_general(
                query, key_tile, (((1,), (1,)), ((), ())), preferred_element_type=jnp.float32
            )
            * score_scale
        )
        allowed = slot < count
        if slot == 0:
            allowed = jnp.logical_and(allowed, cols <= rows)
        masked.append(jnp.where(allowed, scores, -jnp.inf))
    peak = masked[0]
    for scores in masked[1:]:
        peak = jnp.maximum(peak, scores)
    row_peak = jnp.max(peak, axis=1, keepdims=True)
    denominator = jnp.zeros((BLK, 1), jnp.float32)
    weighted = jnp.zeros((BLK, HD), jnp.float32)
    for slot in range(MAXB):
        start = pl.multiple_of(lists_ref[block * MAXB + slot] * BLK, BLK)
        value_tile = v_ref[pl.ds(start, BLK), :]
        exponent = jnp.exp(masked[slot] - row_peak)
        denominator = denominator + jnp.sum(exponent, axis=1, keepdims=True)
        weighted = weighted + jnp.dot(
            exponent.astype(jnp.bfloat16), value_tile, preferred_element_type=jnp.float32
        )
    o_ref[...] = (weighted / denominator).astype(o_ref.dtype)


def attend(lists_flat, counts, head_queries, kv_rows):
    sequence_rows = head_queries.shape[0]
    block_total = sequence_rows // BLK
    return pl.pallas_call(
        attend_kernel,
        out_shape=jax.ShapeDtypeStruct((sequence_rows, HD), jnp.bfloat16),
        grid_spec=pltpu.PrefetchScalarGridSpec(
            num_scalar_prefetch=2,
            grid=(block_total,),
            in_specs=[
                pl.BlockSpec((BLK, HD), lambda i, lists, counts: (i, 0)),
                pl.BlockSpec((sequence_rows, HD), lambda i, lists, counts: (0, 0)),
                pl.BlockSpec((sequence_rows, HD), lambda i, lists, counts: (0, 1)),
            ],
            out_specs=pl.BlockSpec((BLK, HD), lambda i, lists, counts: (i, 0)),
        ),
        compiler_params=pltpu.CompilerParams(dimension_semantics=("arbitrary",)),
    )(lists_flat, counts, head_queries, kv_rows, kv_rows)


def on_device(hidden, norm_gain, queries, key_weight, value_weight, block_lists, block_counts):
    head_queries = lax.all_to_all(queries[0], "ctx", split_axis=1, concat_axis=0, tiled=True)
    upcast = hidden[0].astype(jnp.float32)
    mean_square = jnp.mean(upcast * upcast, axis=-1, keepdims=True)
    normed = (upcast * lax.rsqrt(mean_square + 1e-05) * norm_gain.astype(jnp.float32)).astype(
        jnp.bfloat16
    )
    local_rows, features = normed.shape
    dp_size = lax.axis_size("dp")
    feature_rows = features // dp_size
    feature_split = normed.reshape(local_rows, dp_size, feature_rows).transpose(1, 0, 2)
    gathered = lax.all_to_all(feature_split, "dp", split_axis=0, concat_axis=0, tiled=True)
    local_weight = jnp.concatenate([key_weight, value_weight], axis=1)
    partial = jnp.dot(
        gathered.reshape(dp_size * local_rows, feature_rows),
        local_weight,
        preferred_element_type=jnp.float32,
    ).reshape(dp_size, local_rows, 2 * KVH * HD)
    summed = lax.psum_scatter(partial, "dp", scatter_dimension=0, tiled=True)
    paired = summed.reshape(local_rows, 2, KVH, 1, HD).astype(jnp.bfloat16)
    ctx_size = lax.axis_size("ctx")
    copies_per_head = ctx_size // KVH
    widened = jnp.broadcast_to(paired, (local_rows, 2, KVH, copies_per_head, HD))
    widened = widened.reshape(local_rows, 2, ctx_size, HD)
    head_pair = lax.all_to_all(widened, "ctx", split_axis=2, concat_axis=0, tiled=True)
    sequence_rows = head_queries.shape[0]
    kv_rows = head_pair.reshape(sequence_rows, 2 * HD)
    lists_flat = block_lists[0, 0].reshape(-1)
    counts = block_counts[0, 0]
    attended_head = attend(lists_flat, counts, head_queries, kv_rows)
    restored = lax.all_to_all(attended_head, "ctx", split_axis=0, concat_axis=1, tiled=True)
    return restored[None]


def solution(mesh):
    return jax.shard_map(
        on_device,
        mesh=mesh,
        in_specs=(
            P("dp", "ctx", None),
            P(),
            P("dp", "ctx", None),
            P("dp", None),
            P("dp", None),
            P("dp", "ctx", None, None),
            P("dp", "ctx", None),
        ),
        out_specs=P("dp", "ctx", None),
        check_vma=False,
    )
```

```python
import jax
import jax.numpy as jnp
from jax import lax
from jax.experimental import pallas as pl
from jax.experimental.pallas import tpu as pltpu
from jax.sharding import PartitionSpec as P

KVH = 4
HD = 128
BLK = 128
MAXB = 12


def attend_kernel(lists_ref, counts_ref, q_ref, k_ref, v_ref, o_ref):
    block = pl.program_id(0)
    query = q_ref[...]
    count = counts_ref[block]
    score_scale = HD ** (-0.5)
    rows = lax.broadcasted_iota(jnp.int32, (BLK, BLK), 0)
    cols = lax.broadcasted_iota(jnp.int32, (BLK, BLK), 1)
    masked = []
    for slot in range(MAXB):
        start = pl.multiple_of(lists_ref[block * MAXB + slot] * BLK, BLK)
        key_tile = k_ref[pl.ds(start, BLK), :]
        scores = (
            lax.dot_general(
                query, key_tile, (((1,), (1,)), ((), ())), preferred_element_type=jnp.float32
            )
            * score_scale
        )
        allowed = slot < count
        if slot == 0:
            allowed = jnp.logical_and(allowed, cols <= rows)
        masked.append(jnp.where(allowed, scores, -jnp.inf))
    peak = masked[0]
    for scores in masked[1:]:
        peak = jnp.maximum(peak, scores)
    row_peak = jnp.max(peak, axis=1, keepdims=True)
    denominator = jnp.zeros((BLK, 1), jnp.float32)
    weighted = jnp.zeros((BLK, HD), jnp.float32)
    for slot in range(MAXB):
        start = pl.multiple_of(lists_ref[block * MAXB + slot] * BLK, BLK)
        value_tile = v_ref[pl.ds(start, BLK), :]
        exponent = jnp.exp(masked[slot] - row_peak)
        denominator = denominator + jnp.sum(exponent, axis=1, keepdims=True)
        weighted = weighted + jnp.dot(
            exponent.astype(jnp.bfloat16), value_tile, preferred_element_type=jnp.float32
        )
    o_ref[...] = (weighted / denominator).astype(o_ref.dtype)


def attend(lists_flat, counts, head_queries, kv_rows):
    sequence_rows = head_queries.shape[0]
    block_total = sequence_rows // BLK
    return pl.pallas_call(
        attend_kernel,
        out_shape=jax.ShapeDtypeStruct((sequence_rows, HD), jnp.bfloat16),
        grid_spec=pltpu.PrefetchScalarGridSpec(
            num_scalar_prefetch=2,
            grid=(block_total,),
            in_specs=[
                pl.BlockSpec((BLK, HD), lambda i, lists, counts: (i, 0)),
                pl.BlockSpec((sequence_rows, HD), lambda i, lists, counts: (0, 0)),
                pl.BlockSpec((sequence_rows, HD), lambda i, lists, counts: (0, 1)),
            ],
            out_specs=pl.BlockSpec((BLK, HD), lambda i, lists, counts: (i, 0)),
        ),
        compiler_params=pltpu.CompilerParams(dimension_semantics=("arbitrary",)),
    )(lists_flat, counts, head_queries, kv_rows, kv_rows)


ALL_AXES = ("zh", "core", "x", "y", "zl")
CTX_AXES = ("x", "y", "zl")
DP_AXES = ("zh", "core")


def linear_index(zh, core, x, y, zl):
    return (((zh * 2 + core) * 4 + x) * 4 + y) * 2 + zl


def cross_half_pairs(flip_core):
    pairs = []
    for zh in range(2):
        for core in range(2):
            for x in range(4):
                for y in range(4):
                    for zl in range(2):
                        target_core = 1 - core if flip_core else core
                        pairs.append(
                            (linear_index(zh, core, x, y, zl), linear_index(1 - zh, target_core, x, y, 1 - zl))
                        )
    return pairs


def on_device(hidden, norm_gain, queries, key_weight, value_weight, block_lists, block_counts):
    head_queries = lax.all_to_all(queries[0], CTX_AXES, split_axis=1, concat_axis=0, tiled=True)
    upcast = hidden[0].astype(jnp.float32)
    mean_square = jnp.mean(upcast * upcast, axis=-1, keepdims=True)
    normed = (upcast * lax.rsqrt(mean_square + 1e-05) * norm_gain.astype(jnp.float32)).astype(
        jnp.bfloat16
    )
    local_rows = normed.shape[0]
    local_weight = jnp.concatenate([key_weight, value_weight], axis=1)
    weight_rows = local_weight.shape[0]
    ctx_size = 32
    piece_rows = weight_rows // ctx_size
    ctx_index = lax.axis_index(CTX_AXES)
    piece = lax.dynamic_slice_in_dim(local_weight, (ctx_index ^ 1) * piece_rows, piece_rows, axis=0)
    same_core = lax.ppermute(piece, ALL_AXES, cross_half_pairs(False))
    cross_core = lax.ppermute(piece, ALL_AXES, cross_half_pairs(True))
    other_half = lax.all_gather(
        jnp.stack([same_core, cross_core]), CTX_AXES, axis=1, tiled=True
    )
    sibling = lax.ppermute(local_weight, "core", [(0, 1), (1, 0)])
    zh = lax.axis_index("zh")
    core = lax.axis_index("core")
    blocks = (
        (zh * 2 + core, local_weight),
        (zh * 2 + 1 - core, sibling),
        ((1 - zh) * 2 + core, other_half[0]),
        ((1 - zh) * 2 + 1 - core, other_half[1]),
    )
    summed = None
    for block_index, weight in blocks:
        features = lax.dynamic_slice_in_dim(normed, block_index * weight_rows, weight_rows, axis=1)
        term = jnp.dot(features, weight, preferred_element_type=jnp.float32)
        summed = term if summed is None else summed + term
    paired = summed.astype(jnp.bfloat16).reshape(local_rows, 2, KVH, HD).transpose(2, 0, 1, 3)
    by_group = lax.all_to_all(paired, "x", split_axis=0, concat_axis=0, tiled=True)
    plane = lax.all_gather(by_group, ("y", "zl"), axis=0, tiled=True)
    sequence_rows = head_queries.shape[0]
    kv_rows = plane.reshape(sequence_rows, 2 * HD)
    lists = block_lists[0, 0]
    source = lists // 2
    remapped = (((source % 8) * 4 + source // 8) * 2 + lists % 2).reshape(-1)
    counts = block_counts[0, 0]
    attended_head = attend(remapped, counts, head_queries, kv_rows)
    restored = lax.all_to_all(attended_head, CTX_AXES, split_axis=0, concat_axis=1, tiled=True)
    return restored[None]


def solution(mesh):
    fine = jax.sharding.Mesh(mesh.devices.reshape(2, 2, 4, 4, 2), ALL_AXES)
    return jax.shard_map(
        on_device,
        mesh=fine,
        in_specs=(
            P(DP_AXES, CTX_AXES, None),
            P(),
            P(DP_AXES, CTX_AXES, None),
            P(DP_AXES, None),
            P(DP_AXES, None),
            P(DP_AXES, CTX_AXES, None, None),
            P(DP_AXES, CTX_AXES, None),
        ),
        out_specs=P(DP_AXES, CTX_AXES, None),
        check_vma=False,
    )
```

```python
import jax
import jax.numpy as jnp
from jax import lax
from jax.experimental import pallas as pl
from jax.experimental.pallas import tpu as pltpu
from jax.sharding import PartitionSpec as P

KVH = 4
HD = 128
BLK = 128
MAXB = 12


def attend_kernel(lists_ref, counts_ref, q_ref, k_ref, v_ref, o_ref):
    block = pl.program_id(0)
    query = q_ref[...]
    count = counts_ref[block]
    score_scale = HD ** (-0.5)
    rows = lax.broadcasted_iota(jnp.int32, (BLK, BLK), 0)
    cols = lax.broadcasted_iota(jnp.int32, (BLK, BLK), 1)
    masked = []
    for slot in range(MAXB):
        start = pl.multiple_of(lists_ref[block * MAXB + slot] * BLK, BLK)
        key_tile = k_ref[pl.ds(start, BLK), :]
        scores = (
            lax.dot_general(
                query, key_tile, (((1,), (1,)), ((), ())), preferred_element_type=jnp.float32
            )
            * score_scale
        )
        allowed = slot < count
        if slot == 0:
            allowed = jnp.logical_and(allowed, cols <= rows)
        masked.append(jnp.where(allowed, scores, -jnp.inf))
    peak = masked[0]
    for scores in masked[1:]:
        peak = jnp.maximum(peak, scores)
    row_peak = jnp.max(peak, axis=1, keepdims=True)
    denominator = jnp.zeros((BLK, 1), jnp.float32)
    weighted = jnp.zeros((BLK, HD), jnp.float32)
    for slot in range(MAXB):
        start = pl.multiple_of(lists_ref[block * MAXB + slot] * BLK, BLK)
        value_tile = v_ref[pl.ds(start, BLK), :]
        exponent = jnp.exp(masked[slot] - row_peak)
        denominator = denominator + jnp.sum(exponent, axis=1, keepdims=True)
        weighted = weighted + jnp.dot(
            exponent.astype(jnp.bfloat16), value_tile, preferred_element_type=jnp.float32
        )
    o_ref[...] = (weighted / denominator).astype(o_ref.dtype)


def attend(lists_flat, counts, head_queries, kv_rows):
    sequence_rows = head_queries.shape[0]
    block_total = sequence_rows // BLK
    return pl.pallas_call(
        attend_kernel,
        out_shape=jax.ShapeDtypeStruct((sequence_rows, HD), jnp.bfloat16),
        grid_spec=pltpu.PrefetchScalarGridSpec(
            num_scalar_prefetch=2,
            grid=(block_total,),
            in_specs=[
                pl.BlockSpec((BLK, HD), lambda i, lists, counts: (i, 0)),
                pl.BlockSpec((sequence_rows, HD), lambda i, lists, counts: (0, 0)),
                pl.BlockSpec((sequence_rows, HD), lambda i, lists, counts: (0, 1)),
            ],
            out_specs=pl.BlockSpec((BLK, HD), lambda i, lists, counts: (i, 0)),
        ),
        compiler_params=pltpu.CompilerParams(dimension_semantics=("arbitrary",)),
    )(lists_flat, counts, head_queries, kv_rows, kv_rows)


ALL_AXES = ("zh", "core", "x", "y", "zl")
CTX_AXES = ("x", "y", "zl")
DP_AXES = ("zh", "core")


def linear_index(zh, core, x, y, zl):
    return (((zh * 2 + core) * 4 + x) * 4 + y) * 2 + zl


def cross_half_pairs(flip_core):
    pairs = []
    for zh in range(2):
        for core in range(2):
            for x in range(4):
                for y in range(4):
                    for zl in range(2):
                        target_core = 1 - core if flip_core else core
                        pairs.append(
                            (linear_index(zh, core, x, y, zl), linear_index(1 - zh, target_core, x, y, 1 - zl))
                        )
    return pairs


def on_device(hidden, norm_gain, queries, key_weight, value_weight, block_lists, block_counts):
    head_queries = lax.all_to_all(queries[0], CTX_AXES, split_axis=1, concat_axis=0, tiled=True)
    upcast = hidden[0].astype(jnp.float32)
    mean_square = jnp.mean(upcast * upcast, axis=-1, keepdims=True)
    normed = (upcast * lax.rsqrt(mean_square + 1e-05) * norm_gain.astype(jnp.float32)).astype(
        jnp.bfloat16
    )
    local_rows, features = normed.shape
    local_weight = jnp.concatenate([key_weight, value_weight], axis=1)
    weight_rows = local_weight.shape[0]
    half_features = 2 * weight_rows
    zh = lax.axis_index("zh")
    core = lax.axis_index("core")
    partner_pairs = cross_half_pairs(False)
    far_features = lax.dynamic_slice_in_dim(normed, (1 - zh) * half_features, half_features, axis=1)
    partner_rows = lax.ppermute(far_features, ALL_AXES, partner_pairs)
    sibling = lax.ppermute(local_weight, "core", [(0, 1), (1, 0)])

    def half_sum(rows, offset):
        own = lax.dynamic_slice_in_dim(rows, offset + core * weight_rows, weight_rows, axis=1)
        other = lax.dynamic_slice_in_dim(rows, offset + (1 - core) * weight_rows, weight_rows, axis=1)
        return jnp.dot(own, local_weight, preferred_element_type=jnp.float32) + jnp.dot(
            other, sibling, preferred_element_type=jnp.float32
        )

    for_partner = half_sum(partner_rows, 0)
    from_partner = lax.ppermute(for_partner, ALL_AXES, partner_pairs)
    summed = half_sum(normed, zh * half_features) + from_partner
    paired = summed.reshape(local_rows, 2, KVH, 1, HD).astype(jnp.bfloat16)
    ctx_size = lax.axis_size(CTX_AXES)
    copies_per_head = ctx_size // KVH
    widened = jnp.broadcast_to(paired, (local_rows, 2, KVH, copies_per_head, HD))
    widened = widened.reshape(local_rows, 2, ctx_size, HD)
    head_pair = lax.all_to_all(widened, CTX_AXES, split_axis=2, concat_axis=0, tiled=True)
    sequence_rows = head_queries.shape[0]
    kv_rows = head_pair.reshape(sequence_rows, 2 * HD)
    lists_flat = block_lists[0, 0].reshape(-1)
    counts = block_counts[0, 0]
    attended_head = attend(lists_flat, counts, head_queries, kv_rows)
    restored = lax.all_to_all(attended_head, CTX_AXES, split_axis=0, concat_axis=1, tiled=True)
    return restored[None]


def solution(mesh):
    fine = jax.sharding.Mesh(mesh.devices.reshape(2, 2, 4, 4, 2), ALL_AXES)
    return jax.shard_map(
        on_device,
        mesh=fine,
        in_specs=(
            P(DP_AXES, CTX_AXES, None),
            P(),
            P(DP_AXES, CTX_AXES, None),
            P(DP_AXES, None),
            P(DP_AXES, None),
            P(DP_AXES, CTX_AXES, None, None),
            P(DP_AXES, CTX_AXES, None),
        ),
        out_specs=P(DP_AXES, CTX_AXES, None),
        check_vma=False,
    )
```

```python
import jax
import jax.numpy as jnp
from jax import lax
from jax.experimental import pallas as pl
from jax.experimental.pallas import tpu as pltpu
from jax.sharding import PartitionSpec as P

KVH = 4
HD = 128
BLK = 128
MAXB = 12


SUB_BLOCKS = 8


def attend_kernel(lists_ref, counts_ref, q_ref, kt_ref, v_ref, o_ref):
    step = pl.program_id(0)
    score_scale = HD ** (-0.5)
    rows = lax.broadcasted_iota(jnp.int32, (BLK, BLK), 0)
    cols = lax.broadcasted_iota(jnp.int32, (BLK, BLK), 1)

    def one_block(sub, carry):
        block = step * SUB_BLOCKS + sub
        first_row = pl.multiple_of(sub * BLK, BLK)
        query = q_ref[pl.ds(first_row, BLK), :]
        count = counts_ref[block]
        masked = []
        for slot in range(MAXB):
            start = pl.multiple_of(lists_ref[block * MAXB + slot] * BLK, BLK)
            key_tile = kt_ref[:, pl.ds(start, BLK)]
            scores = jnp.dot(query, key_tile, preferred_element_type=jnp.float32) * score_scale
            allowed = slot < count
            if slot == 0:
                allowed = jnp.logical_and(allowed, cols <= rows)
            masked.append(jnp.where(allowed, scores, -jnp.inf))
        peak = masked[0]
        for scores in masked[1:]:
            peak = jnp.maximum(peak, scores)
        row_peak = jnp.max(peak, axis=1, keepdims=True)
        denominator = jnp.zeros((BLK, 1), jnp.float32)
        weighted = jnp.zeros((BLK, HD), jnp.float32)
        for slot in range(MAXB):
            start = pl.multiple_of(lists_ref[block * MAXB + slot] * BLK, BLK)
            value_tile = v_ref[pl.ds(start, BLK), :]
            exponent = jnp.exp(masked[slot] - row_peak)
            denominator = denominator + jnp.sum(exponent, axis=1, keepdims=True)
            weighted = weighted + jnp.dot(
                exponent.astype(jnp.bfloat16), value_tile, preferred_element_type=jnp.float32
            )
        o_ref[pl.ds(first_row, BLK), :] = (weighted / denominator).astype(o_ref.dtype)
        return carry

    lax.fori_loop(0, SUB_BLOCKS, one_block, 0)


def attend(lists_flat, counts, head_queries, key_t, values):
    sequence_rows = head_queries.shape[0]
    block_total = sequence_rows // BLK
    step_rows = SUB_BLOCKS * BLK
    return pl.pallas_call(
        attend_kernel,
        out_shape=jax.ShapeDtypeStruct((sequence_rows, HD), jnp.bfloat16),
        grid_spec=pltpu.PrefetchScalarGridSpec(
            num_scalar_prefetch=2,
            grid=(block_total // SUB_BLOCKS,),
            in_specs=[
                pl.BlockSpec((step_rows, HD), lambda i, lists, counts: (i, 0)),
                pl.BlockSpec((HD, sequence_rows), lambda i, lists, counts: (0, 0)),
                pl.BlockSpec((sequence_rows, HD), lambda i, lists, counts: (0, 0)),
            ],
            out_specs=pl.BlockSpec((step_rows, HD), lambda i, lists, counts: (i, 0)),
        ),
        compiler_params=pltpu.CompilerParams(dimension_semantics=("arbitrary",)),
    )(lists_flat, counts, head_queries, key_t, values)


ALL_AXES = ("zh", "core", "x", "y", "zl")
CTX_AXES = ("x", "y", "zl")
DP_AXES = ("zh", "core")


def linear_index(zh, core, x, y, zl):
    return (((zh * 2 + core) * 4 + x) * 4 + y) * 2 + zl


def cross_half_pairs(flip_core):
    pairs = []
    for zh in range(2):
        for core in range(2):
            for x in range(4):
                for y in range(4):
                    for zl in range(2):
                        target_core = 1 - core if flip_core else core
                        pairs.append(
                            (linear_index(zh, core, x, y, zl), linear_index(1 - zh, target_core, x, y, 1 - zl))
                        )
    return pairs


def on_device(hidden, norm_gain, queries, key_weight, value_weight, block_lists, block_counts):
    head_queries = lax.all_to_all(queries[0], CTX_AXES, split_axis=1, concat_axis=0, tiled=True)
    upcast = hidden[0].astype(jnp.float32)
    mean_square = jnp.mean(upcast * upcast, axis=-1, keepdims=True)
    normed = (upcast * lax.rsqrt(mean_square + 1e-05) * norm_gain.astype(jnp.float32)).astype(
        jnp.bfloat16
    )
    local_rows, features = normed.shape
    local_weight = jnp.concatenate([key_weight, value_weight], axis=1)
    weight_rows = local_weight.shape[0]
    half_features = 2 * weight_rows
    zh = lax.axis_index("zh")
    core = lax.axis_index("core")
    partner_pairs = cross_half_pairs(False)
    far_features = lax.dynamic_slice_in_dim(normed, (1 - zh) * half_features, half_features, axis=1)
    partner_rows = lax.ppermute(far_features, ALL_AXES, partner_pairs)
    head_queries, partner_rows = lax.optimization_barrier((head_queries, partner_rows))
    sibling = lax.ppermute(local_weight, "core", [(0, 1), (1, 0)])

    def half_sum(rows, offset):
        own = lax.dynamic_slice_in_dim(rows, offset + core * weight_rows, weight_rows, axis=1)
        other = lax.dynamic_slice_in_dim(rows, offset + (1 - core) * weight_rows, weight_rows, axis=1)
        return jnp.dot(own, local_weight, preferred_element_type=jnp.float32) + jnp.dot(
            other, sibling, preferred_element_type=jnp.float32
        )

    for_partner = half_sum(partner_rows, 0)
    from_partner = lax.ppermute(for_partner, ALL_AXES, partner_pairs)
    summed = half_sum(normed, zh * half_features) + from_partner
    paired = summed.reshape(local_rows, 2, KVH, 1, HD).astype(jnp.bfloat16)
    ctx_size = lax.axis_size(CTX_AXES)
    copies_per_head = ctx_size // KVH
    widened = jnp.broadcast_to(paired, (local_rows, 2, KVH, copies_per_head, HD))
    widened = widened.reshape(local_rows, 2, ctx_size, HD)
    head_pair = lax.all_to_all(widened, CTX_AXES, split_axis=2, concat_axis=0, tiled=True)
    sequence_rows = head_queries.shape[0]
    kv_rows = head_pair.reshape(sequence_rows, 2 * HD)
    key_t = kv_rows[:, :HD].T
    values = kv_rows[:, HD:]
    lists_flat = block_lists[0, 0].reshape(-1)
    counts = block_counts[0, 0]
    attended_head = attend(lists_flat, counts, head_queries, key_t, values)
    restored = lax.all_to_all(attended_head, CTX_AXES, split_axis=0, concat_axis=1, tiled=True)
    return restored[None]


def solution(mesh):
    fine = jax.sharding.Mesh(mesh.devices.reshape(2, 2, 4, 4, 2), ALL_AXES)
    return jax.shard_map(
        on_device,
        mesh=fine,
        in_specs=(
            P(DP_AXES, CTX_AXES, None),
            P(),
            P(DP_AXES, CTX_AXES, None),
            P(DP_AXES, None),
            P(DP_AXES, None),
            P(DP_AXES, CTX_AXES, None, None),
            P(DP_AXES, CTX_AXES, None),
        ),
        out_specs=P(DP_AXES, CTX_AXES, None),
        check_vma=False,
    )
```

```python
import functools

import jax
import jax.numpy as jnp
from jax import lax
from jax.experimental import pallas as pl
from jax.experimental.pallas import tpu as pltpu
from jax.sharding import PartitionSpec as P

KVH = 4
HD = 128
BLK = 128
MAXB = 12


SUB_BLOCKS = 8


SUB_BLOCKS = 8


def attend_kernel(parity, lists_ref, counts_ref, q_ref, kt_ref, v_ref, o_ref):
    step = pl.program_id(0)
    score_scale = HD ** (-0.5)
    rows = lax.broadcasted_iota(jnp.int32, (BLK, BLK), 0)
    cols = lax.broadcasted_iota(jnp.int32, (BLK, BLK), 1)

    def one_block(sub, carry):
        block = (step * SUB_BLOCKS + sub) * 2 + parity
        query = q_ref[sub]
        count = counts_ref[block]
        masked = []
        for slot in range(MAXB):
            start = pl.multiple_of(lists_ref[block * MAXB + slot] * BLK, BLK)
            key_tile = kt_ref[:, pl.ds(start, BLK)]
            scores = jnp.dot(query, key_tile, preferred_element_type=jnp.float32) * score_scale
            allowed = slot < count
            if slot == 0:
                allowed = jnp.logical_and(allowed, cols <= rows)
            masked.append(jnp.where(allowed, scores, -jnp.inf))
        peak = masked[0]
        for scores in masked[1:]:
            peak = jnp.maximum(peak, scores)
        row_peak = jnp.max(peak, axis=1, keepdims=True)
        denominator = jnp.zeros((BLK, 1), jnp.float32)
        weighted = jnp.zeros((BLK, HD), jnp.float32)
        for slot in range(MAXB):
            start = pl.multiple_of(lists_ref[block * MAXB + slot] * BLK, BLK)
            value_tile = v_ref[pl.ds(start, BLK), :]
            exponent = jnp.exp(masked[slot] - row_peak)
            denominator = denominator + jnp.sum(exponent, axis=1, keepdims=True)
            weighted = weighted + jnp.dot(
                exponent.astype(jnp.bfloat16), value_tile, preferred_element_type=jnp.float32
            )
        o_ref[sub] = (weighted / denominator).astype(o_ref.dtype)
        return carry

    lax.fori_loop(0, SUB_BLOCKS, one_block, 0)


def attend(parity, lists_flat, counts, query_pairs, key_t, values):
    pair_total = query_pairs.shape[0]
    return pl.pallas_call(
        functools.partial(attend_kernel, parity),
        out_shape=jax.ShapeDtypeStruct((pair_total, BLK, HD), jnp.bfloat16),
        grid_spec=pltpu.PrefetchScalarGridSpec(
            num_scalar_prefetch=2,
            grid=(pair_total // SUB_BLOCKS,),
            in_specs=[
                pl.BlockSpec(
                    (SUB_BLOCKS, None, BLK, HD), lambda i, lists, counts: (i, parity, 0, 0)
                ),
                pl.BlockSpec(key_t.shape, lambda i, lists, counts: (0, 0)),
                pl.BlockSpec(values.shape, lambda i, lists, counts: (0, 0)),
            ],
            out_specs=pl.BlockSpec((SUB_BLOCKS, BLK, HD), lambda i, lists, counts: (i, 0, 0)),
        ),
        compiler_params=pltpu.CompilerParams(dimension_semantics=("arbitrary",)),
    )(lists_flat, counts, query_pairs, key_t, values)


ALL_AXES = ("zh", "core", "x", "y", "zl")
CTX_AXES = ("x", "y", "zl")
DP_AXES = ("zh", "core")


def linear_index(zh, core, x, y, zl):
    return (((zh * 2 + core) * 4 + x) * 4 + y) * 2 + zl


def cross_half_pairs(flip_core):
    pairs = []
    for zh in range(2):
        for core in range(2):
            for x in range(4):
                for y in range(4):
                    for zl in range(2):
                        target_core = 1 - core if flip_core else core
                        pairs.append(
                            (linear_index(zh, core, x, y, zl), linear_index(1 - zh, target_core, x, y, 1 - zl))
                        )
    return pairs


def on_device(hidden, norm_gain, queries, key_weight, value_weight, block_lists, block_counts):
    head_queries = lax.all_to_all(queries[0], CTX_AXES, split_axis=1, concat_axis=0, tiled=True)
    upcast = hidden[0].astype(jnp.float32)
    mean_square = jnp.mean(upcast * upcast, axis=-1, keepdims=True)
    normed = (upcast * lax.rsqrt(mean_square + 1e-05) * norm_gain.astype(jnp.float32)).astype(
        jnp.bfloat16
    )
    local_rows, features = normed.shape
    local_weight = jnp.concatenate([key_weight, value_weight], axis=1)
    weight_rows = local_weight.shape[0]
    half_features = 2 * weight_rows
    zh = lax.axis_index("zh")
    core = lax.axis_index("core")
    partner_pairs = cross_half_pairs(False)
    far_features = lax.dynamic_slice_in_dim(normed, (1 - zh) * half_features, half_features, axis=1)
    partner_rows = lax.ppermute(far_features, ALL_AXES, partner_pairs)
    head_queries, partner_rows = lax.optimization_barrier((head_queries, partner_rows))
    sibling = lax.ppermute(local_weight, "core", [(0, 1), (1, 0)])

    def half_sum(rows, offset):
        own = lax.dynamic_slice_in_dim(rows, offset + core * weight_rows, weight_rows, axis=1)
        other = lax.dynamic_slice_in_dim(rows, offset + (1 - core) * weight_rows, weight_rows, axis=1)
        return jnp.dot(own, local_weight, preferred_element_type=jnp.float32) + jnp.dot(
            other, sibling, preferred_element_type=jnp.float32
        )

    for_partner = half_sum(partner_rows, 0)
    from_partner = lax.ppermute(for_partner, ALL_AXES, partner_pairs)
    summed = half_sum(normed, zh * half_features) + from_partner
    paired = summed.reshape(local_rows, 2, KVH, 1, HD).astype(jnp.bfloat16)
    ctx_size = lax.axis_size(CTX_AXES)
    copies_per_head = ctx_size // KVH
    widened = jnp.broadcast_to(paired, (local_rows, 2, KVH, copies_per_head, HD))
    widened = widened.reshape(local_rows, 2, ctx_size, HD)
    head_pair = lax.all_to_all(widened, CTX_AXES, split_axis=2, concat_axis=0, tiled=True)
    sequence_rows = head_queries.shape[0]
    kv_rows = head_pair.reshape(sequence_rows, 2 * HD)
    key_t = kv_rows[:, :HD].T
    values = kv_rows[:, HD:]
    lists_flat = block_lists[0, 0].reshape(-1)
    counts = block_counts[0, 0]
    query_pairs = head_queries.reshape(sequence_rows // (2 * BLK), 2, BLK, HD)
    halves = []
    for parity in range(2):
        attended_half = attend(parity, lists_flat, counts, query_pairs, key_t, values)
        halves.append(
            lax.all_to_all(
                attended_half.reshape(sequence_rows // 2, HD), CTX_AXES, split_axis=0, concat_axis=1, tiled=True
            )
        )
    restored = jnp.stack(halves).reshape(2 * BLK, -1)
    return restored[None]


def solution(mesh):
    fine = jax.sharding.Mesh(mesh.devices.reshape(2, 2, 4, 4, 2), ALL_AXES)
    return jax.shard_map(
        on_device,
        mesh=fine,
        in_specs=(
            P(DP_AXES, CTX_AXES, None),
            P(),
            P(DP_AXES, CTX_AXES, None),
            P(DP_AXES, None),
            P(DP_AXES, None),
            P(DP_AXES, CTX_AXES, None, None),
            P(DP_AXES, CTX_AXES, None),
        ),
        out_specs=P(DP_AXES, CTX_AXES, None),
        check_vma=False,
    )
```

```python
import jax
import jax.numpy as jnp
from jax import lax
from jax.experimental import pallas as pl
from jax.experimental.pallas import tpu as pltpu
from jax.sharding import PartitionSpec as P

KVH = 4
HD = 128
BLK = 128
MAXB = 12


SUB_BLOCKS = 8


def attend_kernel(lists_ref, counts_ref, q_ref, kt_ref, v_ref, o_ref):
    step = pl.program_id(0)
    score_scale = HD ** (-0.5)
    rows = lax.broadcasted_iota(jnp.int32, (BLK, BLK), 0)
    cols = lax.broadcasted_iota(jnp.int32, (BLK, BLK), 1)

    def one_block(sub, carry):
        block = step * SUB_BLOCKS + sub
        first_row = pl.multiple_of(sub * BLK, BLK)
        query = q_ref[pl.ds(first_row, BLK), :]
        count = counts_ref[block]
        masked = []
        for slot in range(MAXB):
            start = pl.multiple_of(lists_ref[block * MAXB + slot] * BLK, BLK)
            key_tile = kt_ref[:, pl.ds(start, BLK)]
            scores = jnp.dot(query, key_tile, preferred_element_type=jnp.float32) * score_scale
            allowed = slot < count
            if slot == 0:
                allowed = jnp.logical_and(allowed, cols <= rows)
            masked.append(jnp.where(allowed, scores, -jnp.inf))
        peak = masked[0]
        for scores in masked[1:]:
            peak = jnp.maximum(peak, scores)
        row_peak = jnp.max(peak, axis=1, keepdims=True)
        column_sums = jnp.zeros((BLK, BLK), jnp.float32)
        weighted = jnp.zeros((BLK, HD), jnp.float32)
        for slot in range(MAXB):
            start = pl.multiple_of(lists_ref[block * MAXB + slot] * BLK, BLK)
            value_tile = v_ref[pl.ds(start, BLK), :]
            exponent = jnp.exp(masked[slot] - row_peak)
            column_sums = column_sums + exponent
            weighted = weighted + jnp.dot(
                exponent.astype(jnp.bfloat16), value_tile, preferred_element_type=jnp.float32
            )
        denominator = jnp.sum(column_sums, axis=1, keepdims=True)
        o_ref[pl.ds(first_row, BLK), :] = (weighted / denominator).astype(o_ref.dtype)
        return carry

    lax.fori_loop(0, SUB_BLOCKS, one_block, 0, unroll=8)


def attend(lists_flat, counts, head_queries, key_t, values):
    sequence_rows = head_queries.shape[0]
    block_total = sequence_rows // BLK
    step_rows = SUB_BLOCKS * BLK
    return pl.pallas_call(
        attend_kernel,
        out_shape=jax.ShapeDtypeStruct((sequence_rows, HD), jnp.bfloat16),
        grid_spec=pltpu.PrefetchScalarGridSpec(
            num_scalar_prefetch=2,
            grid=(block_total // SUB_BLOCKS,),
            in_specs=[
                pl.BlockSpec((step_rows, HD), lambda i, lists, counts: (i, 0)),
                pl.BlockSpec((HD, sequence_rows), lambda i, lists, counts: (0, 0)),
                pl.BlockSpec((sequence_rows, HD), lambda i, lists, counts: (0, 0)),
            ],
            out_specs=pl.BlockSpec((step_rows, HD), lambda i, lists, counts: (i, 0)),
        ),
        compiler_params=pltpu.CompilerParams(dimension_semantics=("arbitrary",)),
    )(lists_flat, counts, head_queries, key_t, values)


ALL_AXES = ("zh", "core", "x", "y", "zl")
CTX_AXES = ("x", "y", "zl")
DP_AXES = ("zh", "core")


def linear_index(zh, core, x, y, zl):
    return (((zh * 2 + core) * 4 + x) * 4 + y) * 2 + zl


def cross_half_pairs(flip_core):
    pairs = []
    for zh in range(2):
        for core in range(2):
            for x in range(4):
                for y in range(4):
                    for zl in range(2):
                        target_core = 1 - core if flip_core else core
                        pairs.append(
                            (linear_index(zh, core, x, y, zl), linear_index(1 - zh, target_core, x, y, 1 - zl))
                        )
    return pairs


def on_device(hidden, norm_gain, queries, key_weight, value_weight, block_lists, block_counts):
    head_queries = lax.all_to_all(queries[0], CTX_AXES, split_axis=1, concat_axis=0, tiled=True)
    upcast = hidden[0].astype(jnp.float32)
    mean_square = jnp.mean(upcast * upcast, axis=-1, keepdims=True)
    normed = (upcast * lax.rsqrt(mean_square + 1e-05) * norm_gain.astype(jnp.float32)).astype(
        jnp.bfloat16
    )
    local_rows, features = normed.shape
    local_weight = jnp.concatenate([key_weight, value_weight], axis=1)
    weight_rows = local_weight.shape[0]
    half_features = 2 * weight_rows
    zh = lax.axis_index("zh")
    core = lax.axis_index("core")
    partner_pairs = cross_half_pairs(False)
    far_features = lax.dynamic_slice_in_dim(normed, (1 - zh) * half_features, half_features, axis=1)
    partner_rows = lax.ppermute(far_features, ALL_AXES, partner_pairs)
    head_queries, partner_rows = lax.optimization_barrier((head_queries, partner_rows))
    sibling = lax.ppermute(local_weight, "core", [(0, 1), (1, 0)])

    def half_sum(rows, offset):
        own = lax.dynamic_slice_in_dim(rows, offset + core * weight_rows, weight_rows, axis=1)
        other = lax.dynamic_slice_in_dim(rows, offset + (1 - core) * weight_rows, weight_rows, axis=1)
        return jnp.dot(own, local_weight, preferred_element_type=jnp.float32) + jnp.dot(
            other, sibling, preferred_element_type=jnp.float32
        )

    for_partner = half_sum(partner_rows, 0)
    from_partner = lax.ppermute(for_partner, ALL_AXES, partner_pairs)
    summed = half_sum(normed, zh * half_features) + from_partner
    paired = summed.reshape(local_rows, 2, KVH, 1, HD).astype(jnp.bfloat16)
    ctx_size = lax.axis_size(CTX_AXES)
    copies_per_head = ctx_size // KVH
    widened = jnp.broadcast_to(paired, (local_rows, 2, KVH, copies_per_head, HD))
    widened = widened.reshape(local_rows, 2, ctx_size, HD)
    head_pair = lax.all_to_all(widened, CTX_AXES, split_axis=2, concat_axis=0, tiled=True)
    sequence_rows = head_queries.shape[0]
    kv_rows = head_pair.reshape(sequence_rows, 2 * HD)
    key_t = kv_rows[:, :HD].T
    values = kv_rows[:, HD:]
    lists_flat = block_lists[0, 0].reshape(-1)
    counts = block_counts[0, 0]
    attended_head = attend(lists_flat, counts, head_queries, key_t, values)
    restored = lax.all_to_all(attended_head, CTX_AXES, split_axis=0, concat_axis=1, tiled=True)
    return restored[None]


def solution(mesh):
    fine = jax.sharding.Mesh(mesh.devices.reshape(2, 2, 4, 4, 2), ALL_AXES)
    return jax.shard_map(
        on_device,
        mesh=fine,
        in_specs=(
            P(DP_AXES, CTX_AXES, None),
            P(),
            P(DP_AXES, CTX_AXES, None),
            P(DP_AXES, None),
            P(DP_AXES, None),
            P(DP_AXES, CTX_AXES, None, None),
            P(DP_AXES, CTX_AXES, None),
        ),
        out_specs=P(DP_AXES, CTX_AXES, None),
        check_vma=False,
    )
```

```python
import jax
import jax.numpy as jnp
from jax import lax
from jax.experimental import pallas as pl
from jax.experimental.pallas import tpu as pltpu
from jax.sharding import PartitionSpec as P

KVH = 4
HD = 128
BLK = 128
MAXB = 12


SUB_BLOCKS = 8
CHUNKS = 2


def attend_kernel(lists_ref, counts_ref, q_ref, kt_ref, v_ref, o_ref):
    step = pl.program_id(0)
    score_scale = HD ** (-0.5)
    rows = lax.broadcasted_iota(jnp.int32, (BLK, BLK), 0)
    cols = lax.broadcasted_iota(jnp.int32, (BLK, BLK), 1)

    def one_block(sub, carry):
        block = step * SUB_BLOCKS + sub
        first_row = pl.multiple_of(sub * BLK, BLK)
        query = q_ref[pl.ds(first_row, BLK), :]
        count = counts_ref[block]
        masked = []
        for slot in range(MAXB):
            start = pl.multiple_of(lists_ref[block * MAXB + slot] * BLK, BLK)
            key_tile = kt_ref[:, pl.ds(start, BLK)]
            scores = jnp.dot(query, key_tile, preferred_element_type=jnp.float32) * score_scale
            allowed = slot < count
            if slot == 0:
                allowed = jnp.logical_and(allowed, cols <= rows)
            masked.append(jnp.where(allowed, scores, -jnp.inf))
        peak = masked[0]
        for scores in masked[1:]:
            peak = jnp.maximum(peak, scores)
        row_peak = jnp.max(peak, axis=1, keepdims=True)
        column_sums = jnp.zeros((BLK, BLK), jnp.float32)
        weighted = jnp.zeros((BLK, HD), jnp.float32)
        for slot in range(MAXB):
            start = pl.multiple_of(lists_ref[block * MAXB + slot] * BLK, BLK)
            value_tile = v_ref[pl.ds(start, BLK), :]
            exponent = jnp.exp(masked[slot] - row_peak)
            column_sums = column_sums + exponent
            weighted = weighted + jnp.dot(
                exponent.astype(jnp.bfloat16), value_tile, preferred_element_type=jnp.float32
            )
        denominator = jnp.sum(column_sums, axis=1, keepdims=True)
        o_ref[pl.ds(first_row, BLK), :] = (weighted / denominator).astype(o_ref.dtype)
        return carry

    lax.fori_loop(0, SUB_BLOCKS, one_block, 0, unroll=8)


def attend(lists_flat, counts, head_queries, key_t, values):
    sequence_rows = head_queries.shape[0]
    block_total = sequence_rows // BLK
    step_rows = SUB_BLOCKS * BLK
    return pl.pallas_call(
        attend_kernel,
        out_shape=jax.ShapeDtypeStruct((sequence_rows, HD), jnp.bfloat16),
        grid_spec=pltpu.PrefetchScalarGridSpec(
            num_scalar_prefetch=2,
            grid=(block_total // SUB_BLOCKS,),
            in_specs=[
                pl.BlockSpec((step_rows, HD), lambda i, lists, counts: (i, 0)),
                pl.BlockSpec((HD, sequence_rows), lambda i, lists, counts: (0, 0)),
                pl.BlockSpec((sequence_rows, HD), lambda i, lists, counts: (0, 0)),
            ],
            out_specs=pl.BlockSpec((step_rows, HD), lambda i, lists, counts: (i, 0)),
        ),
        compiler_params=pltpu.CompilerParams(dimension_semantics=("arbitrary",)),
    )(lists_flat, counts, head_queries, key_t, values)


ALL_AXES = ("zh", "core", "x", "y", "zl")
CTX_AXES = ("x", "y", "zl")
DP_AXES = ("zh", "core")


def linear_index(zh, core, x, y, zl):
    return (((zh * 2 + core) * 4 + x) * 4 + y) * 2 + zl


def cross_half_pairs(flip_core):
    pairs = []
    for zh in range(2):
        for core in range(2):
            for x in range(4):
                for y in range(4):
                    for zl in range(2):
                        target_core = 1 - core if flip_core else core
                        pairs.append(
                            (linear_index(zh, core, x, y, zl), linear_index(1 - zh, target_core, x, y, 1 - zl))
                        )
    return pairs


def on_device(hidden, norm_gain, queries, key_weight, value_weight, block_lists, block_counts):
    head_queries = lax.all_to_all(queries[0], CTX_AXES, split_axis=1, concat_axis=0, tiled=True)
    upcast = hidden[0].astype(jnp.float32)
    mean_square = jnp.mean(upcast * upcast, axis=-1, keepdims=True)
    normed = (upcast * lax.rsqrt(mean_square + 1e-05) * norm_gain.astype(jnp.float32)).astype(
        jnp.bfloat16
    )
    local_rows, features = normed.shape
    local_weight = jnp.concatenate([key_weight, value_weight], axis=1)
    weight_rows = local_weight.shape[0]
    half_features = 2 * weight_rows
    zh = lax.axis_index("zh")
    core = lax.axis_index("core")
    partner_pairs = cross_half_pairs(False)
    sibling = lax.ppermute(local_weight, "core", [(0, 1), (1, 0)])

    def half_sum(rows, offset):
        own = lax.dynamic_slice_in_dim(rows, offset + core * weight_rows, weight_rows, axis=1)
        other = lax.dynamic_slice_in_dim(rows, offset + (1 - core) * weight_rows, weight_rows, axis=1)
        return jnp.dot(own, local_weight, preferred_element_type=jnp.float32) + jnp.dot(
            other, sibling, preferred_element_type=jnp.float32
        )

    ctx_size = lax.axis_size(CTX_AXES)
    copies_per_head = ctx_size // KVH
    chunk_rows = local_rows // CHUNKS
    kv_chunks = []
    for chunk in range(CHUNKS):
        rows = normed[chunk * chunk_rows : (chunk + 1) * chunk_rows]
        far_features = lax.dynamic_slice_in_dim(rows, (1 - zh) * half_features, half_features, axis=1)
        partner_rows = lax.ppermute(far_features, ALL_AXES, partner_pairs)
        if chunk == 0:
            head_queries, partner_rows = lax.optimization_barrier((head_queries, partner_rows))
        from_partner = lax.ppermute(half_sum(partner_rows, 0), ALL_AXES, partner_pairs)
        summed = half_sum(rows, zh * half_features) + from_partner
        paired = summed.reshape(chunk_rows, 2, KVH, 1, HD).astype(jnp.bfloat16)
        widened = jnp.broadcast_to(paired, (chunk_rows, 2, KVH, copies_per_head, HD))
        widened = widened.reshape(chunk_rows, 2, ctx_size, HD)
        kv_chunks.append(lax.all_to_all(widened, CTX_AXES, split_axis=2, concat_axis=0, tiled=True))
    head_pair = jnp.concatenate(kv_chunks, axis=0)
    sequence_rows = head_queries.shape[0]
    kv_rows = head_pair.reshape(sequence_rows, 2 * HD)
    key_t = kv_rows[:, :HD].T
    values = kv_rows[:, HD:]
    lists = block_lists[0, 0]
    lists_flat = ((lists % CHUNKS) * ctx_size + lists // CHUNKS).reshape(-1)
    counts = block_counts[0, 0]
    attended_head = attend(lists_flat, counts, head_queries, key_t, values)
    restored = lax.all_to_all(attended_head, CTX_AXES, split_axis=0, concat_axis=1, tiled=True)
    return restored[None]


def solution(mesh):
    fine = jax.sharding.Mesh(mesh.devices.reshape(2, 2, 4, 4, 2), ALL_AXES)
    return jax.shard_map(
        on_device,
        mesh=fine,
        in_specs=(
            P(DP_AXES, CTX_AXES, None),
            P(),
            P(DP_AXES, CTX_AXES, None),
            P(DP_AXES, None),
            P(DP_AXES, None),
            P(DP_AXES, CTX_AXES, None, None),
            P(DP_AXES, CTX_AXES, None),
        ),
        out_specs=P(DP_AXES, CTX_AXES, None),
        check_vma=False,
    )
```

```python
import jax
import jax.numpy as jnp
from jax import lax
from jax.experimental import pallas as pl
from jax.experimental.pallas import tpu as pltpu
from jax.sharding import PartitionSpec as P

KVH = 4
HD = 128
BLK = 128
MAXB = 12


SUB_BLOCKS = 8
CHUNKS = 2


def attend_kernel(lists_ref, counts_ref, q_ref, kt_ref, v_ref, o_ref):
    step = pl.program_id(0)
    score_scale = HD ** (-0.5)
    rows = lax.broadcasted_iota(jnp.int32, (BLK, BLK), 0)
    cols = lax.broadcasted_iota(jnp.int32, (BLK, BLK), 1)

    def one_block(sub, carry):
        block = step * SUB_BLOCKS + sub
        first_row = pl.multiple_of(sub * BLK, BLK)
        query = q_ref[pl.ds(first_row, BLK), :]
        count = counts_ref[block]
        masked = []
        for slot in range(MAXB):
            start = pl.multiple_of(lists_ref[block * MAXB + slot] * BLK, BLK)
            key_tile = kt_ref[:, pl.ds(start, BLK)]
            scores = jnp.dot(query, key_tile, preferred_element_type=jnp.float32) * score_scale
            allowed = slot < count
            if slot == 0:
                allowed = jnp.logical_and(allowed, cols <= rows)
            masked.append(jnp.where(allowed, scores, -jnp.inf))
        peak = masked[0]
        for scores in masked[1:]:
            peak = jnp.maximum(peak, scores)
        row_peak = jnp.max(peak, axis=1, keepdims=True)
        column_sums = jnp.zeros((BLK, BLK), jnp.float32)
        weighted = jnp.zeros((BLK, HD), jnp.float32)
        for slot in range(MAXB):
            start = pl.multiple_of(lists_ref[block * MAXB + slot] * BLK, BLK)
            value_tile = v_ref[pl.ds(start, BLK), :]
            exponent = jnp.exp(masked[slot] - row_peak)
            column_sums = column_sums + exponent
            weighted = weighted + jnp.dot(
                exponent.astype(jnp.bfloat16), value_tile, preferred_element_type=jnp.float32
            )
        denominator = jnp.sum(column_sums, axis=1, keepdims=True)
        o_ref[pl.ds(first_row, BLK), :] = (weighted / denominator).astype(o_ref.dtype)
        return carry

    lax.fori_loop(0, SUB_BLOCKS, one_block, 0, unroll=8)


def attend(lists_flat, counts, head_queries, key_t, kv_rows):
    sequence_rows = head_queries.shape[0]
    block_total = sequence_rows // BLK
    step_rows = SUB_BLOCKS * BLK
    return pl.pallas_call(
        attend_kernel,
        out_shape=jax.ShapeDtypeStruct((sequence_rows, HD), jnp.bfloat16),
        grid_spec=pltpu.PrefetchScalarGridSpec(
            num_scalar_prefetch=2,
            grid=(block_total // SUB_BLOCKS,),
            in_specs=[
                pl.BlockSpec((step_rows, HD), lambda i, lists, counts: (i, 0)),
                pl.BlockSpec((HD, sequence_rows), lambda i, lists, counts: (0, 0)),
                pl.BlockSpec((sequence_rows, HD), lambda i, lists, counts: (0, 1)),
            ],
            out_specs=pl.BlockSpec((step_rows, HD), lambda i, lists, counts: (i, 0)),
        ),
        compiler_params=pltpu.CompilerParams(dimension_semantics=("arbitrary",)),
    )(lists_flat, counts, head_queries, key_t, kv_rows)


ALL_AXES = ("zh", "core", "x", "y", "zl")
CTX_AXES = ("x", "y", "zl")
DP_AXES = ("zh", "core")


def linear_index(zh, core, x, y, zl):
    return (((zh * 2 + core) * 4 + x) * 4 + y) * 2 + zl


def cross_half_pairs(flip_core):
    pairs = []
    for zh in range(2):
        for core in range(2):
            for x in range(4):
                for y in range(4):
                    for zl in range(2):
                        target_core = 1 - core if flip_core else core
                        pairs.append(
                            (linear_index(zh, core, x, y, zl), linear_index(1 - zh, target_core, x, y, 1 - zl))
                        )
    return pairs


def on_device(hidden, norm_gain, queries, key_weight, value_weight, block_lists, block_counts):
    head_queries = lax.all_to_all(queries[0], CTX_AXES, split_axis=1, concat_axis=0, tiled=True)
    upcast = hidden[0].astype(jnp.float32)
    mean_square = jnp.mean(upcast * upcast, axis=-1, keepdims=True)
    normed = (upcast * lax.rsqrt(mean_square + 1e-05) * norm_gain.astype(jnp.float32)).astype(
        jnp.bfloat16
    )
    local_rows, features = normed.shape
    local_weight = jnp.concatenate([key_weight, value_weight], axis=1)
    weight_rows = local_weight.shape[0]
    half_features = 2 * weight_rows
    zh = lax.axis_index("zh")
    core = lax.axis_index("core")
    partner_pairs = cross_half_pairs(False)
    sibling = lax.ppermute(local_weight, "core", [(0, 1), (1, 0)])

    def half_sum(rows, offset):
        own = lax.dynamic_slice_in_dim(rows, offset + core * weight_rows, weight_rows, axis=1)
        other = lax.dynamic_slice_in_dim(rows, offset + (1 - core) * weight_rows, weight_rows, axis=1)
        return jnp.dot(own, local_weight, preferred_element_type=jnp.float32) + jnp.dot(
            other, sibling, preferred_element_type=jnp.float32
        )

    ctx_size = lax.axis_size(CTX_AXES)
    copies_per_head = ctx_size // KVH
    chunk_rows = local_rows // CHUNKS
    kv_chunks = []
    for chunk in range(CHUNKS):
        rows = normed[chunk * chunk_rows : (chunk + 1) * chunk_rows]
        far_features = lax.dynamic_slice_in_dim(rows, (1 - zh) * half_features, half_features, axis=1)
        partner_rows = lax.ppermute(far_features, ALL_AXES, partner_pairs)
        if chunk == 0:
            head_queries, partner_rows = lax.optimization_barrier((head_queries, partner_rows))
        for_partner = half_sum(partner_rows, 0).astype(jnp.bfloat16)
        from_partner = lax.ppermute(for_partner, ALL_AXES, partner_pairs)
        summed = half_sum(rows, zh * half_features) + from_partner.astype(jnp.float32)
        paired = summed.reshape(chunk_rows, 2, KVH, 1, HD).astype(jnp.bfloat16)
        widened = jnp.broadcast_to(paired, (chunk_rows, 2, KVH, copies_per_head, HD))
        widened = widened.reshape(chunk_rows, 2, ctx_size, HD)
        kv_chunks.append(lax.all_to_all(widened, CTX_AXES, split_axis=2, concat_axis=0, tiled=True))
    head_pair = jnp.concatenate(kv_chunks, axis=0)
    sequence_rows = head_queries.shape[0]
    kv_rows = head_pair.reshape(sequence_rows, 2 * HD)
    key_t = kv_rows[:, :HD].T
    lists = block_lists[0, 0]
    lists_flat = ((lists % CHUNKS) * ctx_size + lists // CHUNKS).reshape(-1)
    counts = block_counts[0, 0]
    attended_head = attend(lists_flat, counts, head_queries, key_t, kv_rows)
    restored = lax.all_to_all(attended_head, CTX_AXES, split_axis=0, concat_axis=1, tiled=True)
    return restored[None]


def solution(mesh):
    fine = jax.sharding.Mesh(mesh.devices.reshape(2, 2, 4, 4, 2), ALL_AXES)
    return jax.shard_map(
        on_device,
        mesh=fine,
        in_specs=(
            P(DP_AXES, CTX_AXES, None),
            P(),
            P(DP_AXES, CTX_AXES, None),
            P(DP_AXES, None),
            P(DP_AXES, None),
            P(DP_AXES, CTX_AXES, None, None),
            P(DP_AXES, CTX_AXES, None),
        ),
        out_specs=P(DP_AXES, CTX_AXES, None),
        check_vma=False,
    )
```

```python
import jax
import jax.numpy as jnp
from jax import lax
from jax.experimental import pallas as pl
from jax.experimental.pallas import tpu as pltpu
from jax.sharding import PartitionSpec as P

KVH = 4
HD = 128
BLK = 128
MAXB = 12


SUB_BLOCKS = 8
CHUNKS = 2


def attend_kernel(lists_ref, counts_ref, q_ref, kt_ref, v_ref, o_ref):
    step = pl.program_id(0)
    score_scale = HD ** (-0.5)
    rows = lax.broadcasted_iota(jnp.int32, (BLK, BLK), 0)
    cols = lax.broadcasted_iota(jnp.int32, (BLK, BLK), 1)

    def one_block(sub, carry):
        block = step * SUB_BLOCKS + sub
        first_row = pl.multiple_of(sub * BLK, BLK)
        query = q_ref[pl.ds(first_row, BLK), :]
        count = counts_ref[block]
        masked = []
        for slot in range(MAXB):
            start = pl.multiple_of(lists_ref[block * MAXB + slot] * BLK, BLK)
            key_tile = kt_ref[:, pl.ds(start, BLK)]
            scores = jnp.dot(query, key_tile, preferred_element_type=jnp.float32) * score_scale
            allowed = slot < count
            if slot == 0:
                allowed = jnp.logical_and(allowed, cols <= rows)
            masked.append(jnp.where(allowed, scores, -jnp.inf))
        peak = masked[0]
        for scores in masked[1:]:
            peak = jnp.maximum(peak, scores)
        row_peak = jnp.max(peak, axis=1, keepdims=True)
        column_sums = jnp.zeros((BLK, BLK), jnp.float32)
        weighted = jnp.zeros((BLK, HD), jnp.float32)
        for slot in range(MAXB):
            start = pl.multiple_of(lists_ref[block * MAXB + slot] * BLK, BLK)
            value_tile = v_ref[pl.ds(start, BLK), :]
            exponent = jnp.exp(masked[slot] - row_peak)
            column_sums = column_sums + exponent
            weighted = weighted + jnp.dot(
                exponent.astype(jnp.bfloat16), value_tile, preferred_element_type=jnp.float32
            )
        denominator = jnp.sum(column_sums, axis=1, keepdims=True)
        o_ref[pl.ds(first_row, BLK), :] = (weighted / denominator).astype(o_ref.dtype)
        return carry

    lax.fori_loop(0, SUB_BLOCKS, one_block, 0, unroll=8)


def attend(lists_flat, counts, head_queries, key_t, kv_rows):
    sequence_rows = head_queries.shape[0]
    block_total = sequence_rows // BLK
    step_rows = SUB_BLOCKS * BLK
    return pl.pallas_call(
        attend_kernel,
        out_shape=jax.ShapeDtypeStruct((sequence_rows, HD), jnp.bfloat16),
        grid_spec=pltpu.PrefetchScalarGridSpec(
            num_scalar_prefetch=2,
            grid=(block_total // SUB_BLOCKS,),
            in_specs=[
                pl.BlockSpec((step_rows, HD), lambda i, lists, counts: (i, 0)),
                pl.BlockSpec((HD, sequence_rows), lambda i, lists, counts: (0, 0)),
                pl.BlockSpec((sequence_rows, HD), lambda i, lists, counts: (0, 1)),
            ],
            out_specs=pl.BlockSpec((step_rows, HD), lambda i, lists, counts: (i, 0)),
        ),
        compiler_params=pltpu.CompilerParams(dimension_semantics=("arbitrary",)),
    )(lists_flat, counts, head_queries, key_t, kv_rows)


ALL_AXES = ("zh", "core", "x", "y", "zl")
CTX_AXES = ("x", "y", "zl")
DP_AXES = ("zh", "core")


def linear_index(zh, core, x, y, zl):
    return (((zh * 2 + core) * 4 + x) * 4 + y) * 2 + zl


def cross_half_pairs(flip_core):
    pairs = []
    for zh in range(2):
        for core in range(2):
            for x in range(4):
                for y in range(4):
                    for zl in range(2):
                        target_core = 1 - core if flip_core else core
                        pairs.append(
                            (linear_index(zh, core, x, y, zl), linear_index(1 - zh, target_core, x, y, 1 - zl))
                        )
    return pairs


def on_device(hidden, norm_gain, queries, key_weight, value_weight, block_lists, block_counts):
    head_queries = lax.all_to_all(queries[0], CTX_AXES, split_axis=1, concat_axis=0, tiled=True)
    upcast = hidden[0].astype(jnp.float32)
    mean_square = jnp.mean(upcast * upcast, axis=-1, keepdims=True)
    normed = (upcast * lax.rsqrt(mean_square + 1e-05) * norm_gain.astype(jnp.float32)).astype(
        jnp.bfloat16
    )
    local_rows, features = normed.shape
    local_weight = jnp.concatenate([key_weight, value_weight], axis=1)
    weight_rows = local_weight.shape[0]
    half_features = 2 * weight_rows
    zh = lax.axis_index("zh")
    core = lax.axis_index("core")
    partner_pairs = cross_half_pairs(False)
    sibling = lax.ppermute(local_weight, "core", [(0, 1), (1, 0)])

    def half_sum(rows, offset):
        own = lax.dynamic_slice_in_dim(rows, offset + core * weight_rows, weight_rows, axis=1)
        other = lax.dynamic_slice_in_dim(rows, offset + (1 - core) * weight_rows, weight_rows, axis=1)
        return jnp.dot(own, local_weight, preferred_element_type=jnp.float32) + jnp.dot(
            other, sibling, preferred_element_type=jnp.float32
        )

    ctx_size = lax.axis_size(CTX_AXES)
    copies_per_head = ctx_size // KVH
    chunk_rows = local_rows // CHUNKS
    kv_chunks = []
    own_half = half_sum(normed, zh * half_features)
    for chunk in range(CHUNKS):
        rows = normed[chunk * chunk_rows : (chunk + 1) * chunk_rows]
        far_features = lax.dynamic_slice_in_dim(rows, (1 - zh) * half_features, half_features, axis=1)
        partner_rows = lax.ppermute(far_features, ALL_AXES, partner_pairs)
        if chunk == 0:
            head_queries, partner_rows = lax.optimization_barrier((head_queries, partner_rows))
        from_partner = lax.ppermute(half_sum(partner_rows, 0), ALL_AXES, partner_pairs)
        summed = own_half[chunk * chunk_rows : (chunk + 1) * chunk_rows] + from_partner
        paired = summed.reshape(chunk_rows, 2, KVH, 1, HD).astype(jnp.bfloat16)
        widened = jnp.broadcast_to(paired, (chunk_rows, 2, KVH, copies_per_head, HD))
        widened = widened.reshape(chunk_rows, 2, ctx_size, HD)
        kv_chunks.append(lax.all_to_all(widened, CTX_AXES, split_axis=2, concat_axis=0, tiled=True))
    head_pair = jnp.concatenate(kv_chunks, axis=0)
    sequence_rows = head_queries.shape[0]
    kv_rows = head_pair.reshape(sequence_rows, 2 * HD)
    key_t = kv_rows[:, :HD].T
    lists = block_lists[0, 0]
    lists_flat = ((lists % CHUNKS) * ctx_size + lists // CHUNKS).reshape(-1)
    counts = block_counts[0, 0]
    attended_head = attend(lists_flat, counts, head_queries, key_t, kv_rows)
    restored = lax.all_to_all(attended_head, CTX_AXES, split_axis=0, concat_axis=1, tiled=True)
    return restored[None]


def solution(mesh):
    fine = jax.sharding.Mesh(mesh.devices.reshape(2, 2, 4, 4, 2), ALL_AXES)
    return jax.shard_map(
        on_device,
        mesh=fine,
        in_specs=(
            P(DP_AXES, CTX_AXES, None),
            P(),
            P(DP_AXES, CTX_AXES, None),
            P(DP_AXES, None),
            P(DP_AXES, None),
            P(DP_AXES, CTX_AXES, None, None),
            P(DP_AXES, CTX_AXES, None),
        ),
        out_specs=P(DP_AXES, CTX_AXES, None),
        check_vma=False,
    )
```

```python
import jax
import jax.numpy as jnp
from jax import lax
from jax.experimental import pallas as pl
from jax.experimental.pallas import tpu as pltpu
from jax.sharding import PartitionSpec as P

KVH = 4
HD = 128
BLK = 128
MAXB = 12


SUB_BLOCKS = 8
CHUNKS = 2


def attend_kernel(lists_ref, counts_ref, q_ref, kt_ref, v_ref, o_ref):
    step = pl.program_id(0)
    score_scale = HD ** (-0.5)
    rows = lax.broadcasted_iota(jnp.int32, (BLK, BLK), 0)
    cols = lax.broadcasted_iota(jnp.int32, (BLK, BLK), 1)

    def one_block(sub, carry):
        block = step * SUB_BLOCKS + sub
        first_row = pl.multiple_of(sub * BLK, BLK)
        query = q_ref[pl.ds(first_row, BLK), :]
        count = counts_ref[block]
        masked = []
        for slot in range(MAXB):
            start = pl.multiple_of(lists_ref[block * MAXB + slot] * BLK, BLK)
            key_tile = kt_ref[:, pl.ds(start, BLK)]
            scores = jnp.dot(query, key_tile, preferred_element_type=jnp.float32) * score_scale
            allowed = slot < count
            if slot == 0:
                allowed = jnp.logical_and(allowed, cols <= rows)
            masked.append(jnp.where(allowed, scores, -jnp.inf))
        peak = masked[0]
        for scores in masked[1:]:
            peak = jnp.maximum(peak, scores)
        row_peak = jnp.max(peak, axis=1, keepdims=True)
        column_sums = jnp.zeros((BLK, BLK), jnp.float32)
        weighted = jnp.zeros((BLK, HD), jnp.float32)
        for slot in range(MAXB):
            start = pl.multiple_of(lists_ref[block * MAXB + slot] * BLK, BLK)
            value_tile = v_ref[pl.ds(start, BLK), :]
            exponent = jnp.exp(masked[slot] - row_peak)
            column_sums = column_sums + exponent
            weighted = weighted + jnp.dot(
                exponent.astype(jnp.bfloat16), value_tile, preferred_element_type=jnp.float32
            )
        denominator = jnp.sum(column_sums, axis=1, keepdims=True)
        o_ref[pl.ds(first_row, BLK), :] = (weighted / denominator).astype(o_ref.dtype)
        return carry

    lax.fori_loop(0, SUB_BLOCKS, one_block, 0, unroll=8)


def attend(lists_flat, counts, head_queries, key_t, kv_rows):
    sequence_rows = head_queries.shape[0]
    block_total = sequence_rows // BLK
    step_rows = SUB_BLOCKS * BLK
    return pl.pallas_call(
        attend_kernel,
        out_shape=jax.ShapeDtypeStruct((sequence_rows, HD), jnp.bfloat16),
        grid_spec=pltpu.PrefetchScalarGridSpec(
            num_scalar_prefetch=2,
            grid=(block_total // SUB_BLOCKS,),
            in_specs=[
                pl.BlockSpec((step_rows, HD), lambda i, lists, counts: (i, 0)),
                pl.BlockSpec((HD, sequence_rows), lambda i, lists, counts: (0, 0)),
                pl.BlockSpec((sequence_rows, HD), lambda i, lists, counts: (0, 1)),
            ],
            out_specs=pl.BlockSpec((step_rows, HD), lambda i, lists, counts: (i, 0)),
        ),
        compiler_params=pltpu.CompilerParams(dimension_semantics=("arbitrary",)),
    )(lists_flat, counts, head_queries, key_t, kv_rows)


ALL_AXES = ("zh", "core", "x", "y", "zl")
CTX_AXES = ("x", "y", "zl")
DP_AXES = ("zh", "core")


def linear_index(zh, core, x, y, zl):
    return (((zh * 2 + core) * 4 + x) * 4 + y) * 2 + zl


def cross_half_pairs(flip_core):
    pairs = []
    for zh in range(2):
        for core in range(2):
            for x in range(4):
                for y in range(4):
                    for zl in range(2):
                        target_core = 1 - core if flip_core else core
                        pairs.append(
                            (linear_index(zh, core, x, y, zl), linear_index(1 - zh, target_core, x, y, 1 - zl))
                        )
    return pairs


def on_device(hidden, norm_gain, queries, key_weight, value_weight, block_lists, block_counts):
    head_queries = lax.all_to_all(queries[0], CTX_AXES, split_axis=1, concat_axis=0, tiled=True)
    upcast = hidden[0].astype(jnp.float32)
    mean_square = jnp.mean(upcast * upcast, axis=-1, keepdims=True)
    normed = (upcast * lax.rsqrt(mean_square + 1e-05) * norm_gain.astype(jnp.float32)).astype(
        jnp.bfloat16
    )
    local_rows, features = normed.shape
    local_weight = jnp.concatenate([key_weight, value_weight], axis=1)
    weight_rows = local_weight.shape[0]
    half_features = 2 * weight_rows
    zh = lax.axis_index("zh")
    core = lax.axis_index("core")
    partner_pairs = cross_half_pairs(False)
    sibling = lax.ppermute(local_weight, "core", [(0, 1), (1, 0)])

    def half_sum(rows, offset):
        own = lax.dynamic_slice_in_dim(rows, offset + core * weight_rows, weight_rows, axis=1)
        other = lax.dynamic_slice_in_dim(rows, offset + (1 - core) * weight_rows, weight_rows, axis=1)
        return jnp.dot(own, local_weight, preferred_element_type=jnp.float32) + jnp.dot(
            other, sibling, preferred_element_type=jnp.float32
        )

    ctx_size = lax.axis_size(CTX_AXES)
    copies_per_head = ctx_size // KVH
    chunk_rows = local_rows // CHUNKS
    kv_chunks = []
    for chunk in range(CHUNKS):
        rows = normed[chunk * chunk_rows : (chunk + 1) * chunk_rows]
        far_features = lax.dynamic_slice_in_dim(rows, (1 - zh) * half_features, half_features, axis=1)
        partner_rows = lax.ppermute(far_features, ALL_AXES, partner_pairs)
        if chunk == 0:
            head_queries, partner_rows = lax.optimization_barrier((head_queries, partner_rows))
        from_partner = lax.ppermute(half_sum(partner_rows, 0), ALL_AXES, partner_pairs)
        summed = half_sum(rows, zh * half_features) + from_partner
        paired = summed.reshape(chunk_rows, 2, KVH, 1, HD).astype(jnp.bfloat16)
        widened = jnp.broadcast_to(paired, (chunk_rows, 2, KVH, copies_per_head, HD))
        widened = widened.reshape(chunk_rows, 2, ctx_size, HD)
        kv_chunks.append(lax.all_to_all(widened, CTX_AXES, split_axis=2, concat_axis=0, tiled=True))
    head_pair = jnp.concatenate(kv_chunks, axis=0)
    sequence_rows = head_queries.shape[0]
    kv_rows = head_pair.reshape(sequence_rows, 2 * HD)
    key_t = kv_rows[:, :HD].T
    lists = block_lists[0, 0]
    lists_flat = ((lists % CHUNKS) * ctx_size + lists // CHUNKS).reshape(-1)
    counts = block_counts[0, 0]
    attended_head = attend(lists_flat, counts, head_queries, key_t, kv_rows)
    restored = lax.all_to_all(attended_head, CTX_AXES, split_axis=0, concat_axis=1, tiled=True)
    return restored[None]


def solution(mesh):
    fine = jax.sharding.Mesh(mesh.devices.reshape(2, 2, 4, 4, 2), ALL_AXES)
    return jax.shard_map(
        on_device,
        mesh=fine,
        in_specs=(
            P(DP_AXES, CTX_AXES, None),
            P(),
            P(DP_AXES, CTX_AXES, None),
            P(DP_AXES, None),
            P(DP_AXES, None),
            P(DP_AXES, CTX_AXES, None, None),
            P(DP_AXES, CTX_AXES, None),
        ),
        out_specs=P(DP_AXES, CTX_AXES, None),
        check_vma=False,
    )
```

```python
import jax
import jax.numpy as jnp
from jax import lax
from jax.experimental import pallas as pl
from jax.experimental.pallas import tpu as pltpu
from jax.sharding import PartitionSpec as P

KVH = 4
HD = 128
BLK = 128
MAXB = 12


SUB_BLOCKS = 8
CHUNKS = 2


def attend_kernel(lists_ref, counts_ref, q_ref, kt_ref, v_ref, o_ref):
    step = pl.program_id(0)
    score_scale = HD ** (-0.5)
    rows = lax.broadcasted_iota(jnp.int32, (BLK, BLK), 0)
    cols = lax.broadcasted_iota(jnp.int32, (BLK, BLK), 1)

    def one_block(sub, carry):
        block = step * SUB_BLOCKS + sub
        first_row = pl.multiple_of(sub * BLK, BLK)
        query = q_ref[pl.ds(first_row, BLK), :]
        count = counts_ref[block]
        masked = []
        for slot in range(MAXB):
            start = pl.multiple_of(lists_ref[block * MAXB + slot] * BLK, BLK)
            key_tile = kt_ref[:, pl.ds(start, BLK)]
            scores = jnp.dot(query, key_tile, preferred_element_type=jnp.float32) * score_scale
            allowed = slot < count
            if slot == 0:
                allowed = jnp.logical_and(allowed, cols <= rows)
            masked.append(jnp.where(allowed, scores, -jnp.inf))
        peak = masked[0]
        for scores in masked[1:]:
            peak = jnp.maximum(peak, scores)
        row_peak = jnp.max(peak, axis=1, keepdims=True)
        column_sums = jnp.zeros((BLK, BLK), jnp.float32)
        weighted = jnp.zeros((BLK, HD), jnp.float32)
        for slot in range(MAXB):
            start = pl.multiple_of(lists_ref[block * MAXB + slot] * BLK, BLK)
            value_tile = v_ref[pl.ds(start, BLK), :]
            exponent = jnp.exp(masked[slot] - row_peak)
            column_sums = column_sums + exponent
            weighted = weighted + jnp.dot(
                exponent.astype(jnp.bfloat16), value_tile, preferred_element_type=jnp.float32
            )
        denominator = jnp.sum(column_sums, axis=1, keepdims=True)
        o_ref[pl.ds(first_row, BLK), :] = (weighted / denominator).astype(o_ref.dtype)
        return carry

    lax.fori_loop(0, SUB_BLOCKS, one_block, 0, unroll=8)


def attend(lists_flat, counts, head_queries, key_t, kv_rows):
    sequence_rows = head_queries.shape[0]
    block_total = sequence_rows // BLK
    step_rows = SUB_BLOCKS * BLK
    return pl.pallas_call(
        attend_kernel,
        out_shape=jax.ShapeDtypeStruct((sequence_rows, HD), jnp.bfloat16),
        grid_spec=pltpu.PrefetchScalarGridSpec(
            num_scalar_prefetch=2,
            grid=(block_total // SUB_BLOCKS,),
            in_specs=[
                pl.BlockSpec((step_rows, HD), lambda i, lists, counts: (i, 0)),
                pl.BlockSpec((HD, sequence_rows), lambda i, lists, counts: (0, 0)),
                pl.BlockSpec((sequence_rows, HD), lambda i, lists, counts: (0, 1)),
            ],
            out_specs=pl.BlockSpec((step_rows, HD), lambda i, lists, counts: (i, 0)),
        ),
        compiler_params=pltpu.CompilerParams(dimension_semantics=("arbitrary",)),
    )(lists_flat, counts, head_queries, key_t, kv_rows)


ALL_AXES = ("zh", "core", "x", "y", "zl")
CTX_AXES = ("x", "y", "zl")
DP_AXES = ("zh", "core")


def linear_index(zh, core, x, y, zl):
    return (((zh * 2 + core) * 4 + x) * 4 + y) * 2 + zl


def cross_half_pairs(flip_core):
    pairs = []
    for zh in range(2):
        for core in range(2):
            for x in range(4):
                for y in range(4):
                    for zl in range(2):
                        target_core = 1 - core if flip_core else core
                        pairs.append(
                            (linear_index(zh, core, x, y, zl), linear_index(1 - zh, target_core, x, y, 1 - zl))
                        )
    return pairs


def on_device(hidden, norm_gain, queries, key_weight, value_weight, block_lists, block_counts):
    upcast = hidden[0].astype(jnp.float32)
    mean_square = jnp.mean(upcast * upcast, axis=-1, keepdims=True)
    normed = (upcast * lax.rsqrt(mean_square + 1e-05) * norm_gain.astype(jnp.float32)).astype(
        jnp.bfloat16
    )
    local_rows, features = normed.shape
    local_weight = jnp.concatenate([key_weight, value_weight], axis=1)
    weight_rows = local_weight.shape[0]
    half_features = 2 * weight_rows
    zh = lax.axis_index("zh")
    core = lax.axis_index("core")
    partner_pairs = cross_half_pairs(False)
    sibling = lax.ppermute(local_weight, "core", [(0, 1), (1, 0)])

    def half_sum(rows, offset):
        own = lax.dynamic_slice_in_dim(rows, offset + core * weight_rows, weight_rows, axis=1)
        other = lax.dynamic_slice_in_dim(rows, offset + (1 - core) * weight_rows, weight_rows, axis=1)
        return jnp.dot(own, local_weight, preferred_element_type=jnp.float32) + jnp.dot(
            other, sibling, preferred_element_type=jnp.float32
        )

    ctx_size = lax.axis_size(CTX_AXES)
    copies_per_head = ctx_size // KVH
    chunk_rows = local_rows // CHUNKS
    kv_chunks = []
    for chunk in range(CHUNKS):
        rows = normed[chunk * chunk_rows : (chunk + 1) * chunk_rows]
        far_features = lax.dynamic_slice_in_dim(rows, (1 - zh) * half_features, half_features, axis=1)
        partner_rows = lax.ppermute(far_features, ALL_AXES, partner_pairs)
        if chunk == 0:
            local_queries, partner_rows = lax.optimization_barrier((queries[0], partner_rows))
            head_queries = lax.all_to_all(local_queries, CTX_AXES, split_axis=1, concat_axis=0, tiled=True)
        from_partner = lax.ppermute(half_sum(partner_rows, 0), ALL_AXES, partner_pairs)
        summed = half_sum(rows, zh * half_features) + from_partner
        paired = summed.reshape(chunk_rows, 2, KVH, 1, HD).astype(jnp.bfloat16)
        widened = jnp.broadcast_to(paired, (chunk_rows, 2, KVH, copies_per_head, HD))
        widened = widened.reshape(chunk_rows, 2, ctx_size, HD)
        if chunk == 0:
            head_queries, widened = lax.optimization_barrier((head_queries, widened))
        kv_chunks.append(lax.all_to_all(widened, CTX_AXES, split_axis=2, concat_axis=0, tiled=True))
    head_pair = jnp.concatenate(kv_chunks, axis=0)
    sequence_rows = head_queries.shape[0]
    kv_rows = head_pair.reshape(sequence_rows, 2 * HD)
    key_t = kv_rows[:, :HD].T
    lists = block_lists[0, 0]
    lists_flat = ((lists % CHUNKS) * ctx_size + lists // CHUNKS).reshape(-1)
    counts = block_counts[0, 0]
    attended_head = attend(lists_flat, counts, head_queries, key_t, kv_rows)
    restored = lax.all_to_all(attended_head, CTX_AXES, split_axis=0, concat_axis=1, tiled=True)
    return restored[None]


def solution(mesh):
    fine = jax.sharding.Mesh(mesh.devices.reshape(2, 2, 4, 4, 2), ALL_AXES)
    return jax.shard_map(
        on_device,
        mesh=fine,
        in_specs=(
            P(DP_AXES, CTX_AXES, None),
            P(),
            P(DP_AXES, CTX_AXES, None),
            P(DP_AXES, None),
            P(DP_AXES, None),
            P(DP_AXES, CTX_AXES, None, None),
            P(DP_AXES, CTX_AXES, None),
        ),
        out_specs=P(DP_AXES, CTX_AXES, None),
        check_vma=False,
    )
```

```python
import jax
import jax.numpy as jnp
from jax import lax
from jax.experimental import pallas as pl
from jax.experimental.pallas import tpu as pltpu
from jax.sharding import PartitionSpec as P

KVH = 4
HD = 128
BLK = 128
MAXB = 12


SUB_BLOCKS = 8
CHUNKS = 2


def attend_kernel(lists_ref, counts_ref, q_ref, kt_ref, v_ref, o_ref):
    step = pl.program_id(0)
    score_scale = HD ** (-0.5)
    rows = lax.broadcasted_iota(jnp.int32, (BLK, BLK), 0)
    cols = lax.broadcasted_iota(jnp.int32, (BLK, BLK), 1)

    def one_block(sub, carry):
        block = step * SUB_BLOCKS + sub
        first_row = pl.multiple_of(sub * BLK, BLK)
        query = q_ref[pl.ds(first_row, BLK), :]
        count = counts_ref[block]
        masked = []
        for slot in range(MAXB):
            start = pl.multiple_of(lists_ref[block * MAXB + slot] * BLK, BLK)
            key_tile = kt_ref[:, pl.ds(start, BLK)]
            scores = jnp.dot(query, key_tile, preferred_element_type=jnp.float32) * score_scale
            allowed = slot < count
            if slot == 0:
                allowed = jnp.logical_and(allowed, cols <= rows)
            masked.append(jnp.where(allowed, scores, -jnp.inf))
        peak = masked[0]
        for scores in masked[1:]:
            peak = jnp.maximum(peak, scores)
        row_peak = jnp.max(peak, axis=1, keepdims=True)
        column_sums = jnp.zeros((BLK, BLK), jnp.float32)
        weighted = jnp.zeros((BLK, HD), jnp.float32)
        for slot in range(MAXB):
            start = pl.multiple_of(lists_ref[block * MAXB + slot] * BLK, BLK)
            value_tile = v_ref[pl.ds(start, BLK), :]
            exponent = jnp.exp(masked[slot] - row_peak)
            column_sums = column_sums + exponent
            weighted = weighted + jnp.dot(
                exponent.astype(jnp.bfloat16), value_tile, preferred_element_type=jnp.float32
            )
        denominator = jnp.sum(column_sums, axis=1, keepdims=True)
        o_ref[pl.ds(first_row, BLK), :] = (weighted / denominator).astype(o_ref.dtype)
        return carry

    lax.fori_loop(0, SUB_BLOCKS, one_block, 0, unroll=8)


def attend(lists_flat, counts, head_queries, key_t, kv_rows):
    sequence_rows = head_queries.shape[0]
    block_total = sequence_rows // BLK
    step_rows = SUB_BLOCKS * BLK
    return pl.pallas_call(
        attend_kernel,
        out_shape=jax.ShapeDtypeStruct((sequence_rows, HD), jnp.bfloat16),
        grid_spec=pltpu.PrefetchScalarGridSpec(
            num_scalar_prefetch=2,
            grid=(block_total // SUB_BLOCKS,),
            in_specs=[
                pl.BlockSpec((step_rows, HD), lambda i, lists, counts: (i, 0)),
                pl.BlockSpec((HD, sequence_rows), lambda i, lists, counts: (0, 0)),
                pl.BlockSpec((sequence_rows, HD), lambda i, lists, counts: (0, 0)),
            ],
            out_specs=pl.BlockSpec((step_rows, HD), lambda i, lists, counts: (i, 0)),
        ),
        compiler_params=pltpu.CompilerParams(dimension_semantics=("arbitrary",)),
    )(lists_flat, counts, head_queries, key_t, kv_rows)


ALL_AXES = ("zh", "core", "x", "y", "zl")
CTX_AXES = ("x", "y", "zl")
DP_AXES = ("zh", "core")


def linear_index(zh, core, x, y, zl):
    return (((zh * 2 + core) * 4 + x) * 4 + y) * 2 + zl


def cross_half_pairs(flip_core):
    pairs = []
    for zh in range(2):
        for core in range(2):
            for x in range(4):
                for y in range(4):
                    for zl in range(2):
                        target_core = 1 - core if flip_core else core
                        pairs.append(
                            (linear_index(zh, core, x, y, zl), linear_index(1 - zh, target_core, x, y, 1 - zl))
                        )
    return pairs


def on_device(hidden, norm_gain, queries, key_weight, value_weight, block_lists, block_counts):
    head_queries = lax.all_to_all(queries[0], CTX_AXES, split_axis=1, concat_axis=0, tiled=True)
    upcast = hidden[0].astype(jnp.float32)
    mean_square = jnp.mean(upcast * upcast, axis=-1, keepdims=True)
    normed = (upcast * lax.rsqrt(mean_square + 1e-05) * norm_gain.astype(jnp.float32)).astype(
        jnp.bfloat16
    )
    local_rows, features = normed.shape
    local_weight = jnp.concatenate([key_weight, value_weight], axis=1)
    weight_rows = local_weight.shape[0]
    half_features = 2 * weight_rows
    zh = lax.axis_index("zh")
    core = lax.axis_index("core")
    partner_pairs = cross_half_pairs(False)
    sibling = lax.ppermute(local_weight, "core", [(0, 1), (1, 0)])

    def half_sum(rows, offset):
        own = lax.dynamic_slice_in_dim(rows, offset + core * weight_rows, weight_rows, axis=1)
        other = lax.dynamic_slice_in_dim(rows, offset + (1 - core) * weight_rows, weight_rows, axis=1)
        return jnp.dot(own, local_weight, preferred_element_type=jnp.float32) + jnp.dot(
            other, sibling, preferred_element_type=jnp.float32
        )

    ctx_size = lax.axis_size(CTX_AXES)
    copies_per_head = ctx_size // KVH
    chunk_rows = local_rows // CHUNKS
    kv_chunks = []
    for chunk in range(CHUNKS):
        rows = normed[chunk * chunk_rows : (chunk + 1) * chunk_rows]
        far_features = lax.dynamic_slice_in_dim(rows, (1 - zh) * half_features, half_features, axis=1)
        partner_rows = lax.ppermute(far_features, ALL_AXES, partner_pairs)
        if chunk == 0:
            head_queries, partner_rows = lax.optimization_barrier((head_queries, partner_rows))
        from_partner = lax.ppermute(half_sum(partner_rows, 0), ALL_AXES, partner_pairs)
        summed = half_sum(rows, zh * half_features) + from_partner
        paired = summed.reshape(chunk_rows, 2, KVH, 1, HD).astype(jnp.bfloat16)
        widened = jnp.broadcast_to(paired, (chunk_rows, 2, KVH, copies_per_head, HD))
        widened = widened.reshape(chunk_rows, 2, ctx_size, HD)
        arrived = lax.all_to_all(widened, CTX_AXES, split_axis=2, concat_axis=0, tiled=True)
        kv_chunks.append(arrived.reshape(ctx_size * chunk_rows, 2 * HD))
    if CHUNKS > 1:
        early_key_t, early_values = lax.optimization_barrier(
            (kv_chunks[0][:, :HD].T, kv_chunks[0][:, HD:])
        )
    sequence_rows = head_queries.shape[0]
    key_t = jnp.concatenate([early_key_t] + [part[:, :HD].T for part in kv_chunks[1:]], axis=1)
    kv_rows = jnp.concatenate([early_values] + [part[:, HD:] for part in kv_chunks[1:]], axis=0)
    lists = block_lists[0, 0]
    lists_flat = ((lists % CHUNKS) * ctx_size + lists // CHUNKS).reshape(-1)
    counts = block_counts[0, 0]
    attended_head = attend(lists_flat, counts, head_queries, key_t, kv_rows)
    restored = lax.all_to_all(attended_head, CTX_AXES, split_axis=0, concat_axis=1, tiled=True)
    return restored[None]


def solution(mesh):
    fine = jax.sharding.Mesh(mesh.devices.reshape(2, 2, 4, 4, 2), ALL_AXES)
    return jax.shard_map(
        on_device,
        mesh=fine,
        in_specs=(
            P(DP_AXES, CTX_AXES, None),
            P(),
            P(DP_AXES, CTX_AXES, None),
            P(DP_AXES, None),
            P(DP_AXES, None),
            P(DP_AXES, CTX_AXES, None, None),
            P(DP_AXES, CTX_AXES, None),
        ),
        out_specs=P(DP_AXES, CTX_AXES, None),
        check_vma=False,
    )
```

```python
import jax
import jax.numpy as jnp
from jax import lax
from jax.experimental import pallas as pl
from jax.experimental.pallas import tpu as pltpu
from jax.sharding import PartitionSpec as P

KVH = 4
HD = 128
BLK = 128
MAXB = 12


SUB_BLOCKS = 8
CHUNKS = 2


def attend_kernel(lists_ref, counts_ref, q_ref, kt_ref, v_ref, o_ref):
    step = pl.program_id(0)
    score_scale = HD ** (-0.5)
    rows = lax.broadcasted_iota(jnp.int32, (BLK, BLK), 0)
    cols = lax.broadcasted_iota(jnp.int32, (BLK, BLK), 1)

    def one_block(sub, carry):
        block = step * SUB_BLOCKS + sub
        first_row = pl.multiple_of(sub * BLK, BLK)
        query = q_ref[pl.ds(first_row, BLK), :]
        count = counts_ref[block]
        masked = []
        for slot in range(MAXB):
            start = pl.multiple_of(lists_ref[block * MAXB + slot] * BLK, BLK)
            key_tile = kt_ref[:, pl.ds(start, BLK)]
            scores = jnp.dot(query, key_tile, preferred_element_type=jnp.float32) * score_scale
            allowed = slot < count
            if slot == 0:
                allowed = jnp.logical_and(allowed, cols <= rows)
            masked.append(jnp.where(allowed, scores, -jnp.inf))
        peak = masked[0]
        for scores in masked[1:]:
            peak = jnp.maximum(peak, scores)
        row_peak = jnp.max(peak, axis=1, keepdims=True)
        column_sums = jnp.zeros((BLK, BLK), jnp.float32)
        weighted = jnp.zeros((BLK, HD), jnp.float32)
        for slot in range(MAXB):
            start = pl.multiple_of(lists_ref[block * MAXB + slot] * BLK, BLK)
            value_tile = v_ref[pl.ds(start, BLK), :]
            exponent = jnp.exp(masked[slot] - row_peak)
            column_sums = column_sums + exponent
            weighted = weighted + jnp.dot(
                exponent.astype(jnp.bfloat16), value_tile, preferred_element_type=jnp.float32
            )
        denominator = jnp.sum(column_sums, axis=1, keepdims=True)
        o_ref[pl.ds(first_row, BLK), :] = (weighted / denominator).astype(o_ref.dtype)
        return carry

    lax.fori_loop(0, SUB_BLOCKS, one_block, 0, unroll=8)


def attend(lists_flat, counts, head_queries, key_t, kv_rows):
    sequence_rows = head_queries.shape[0]
    block_total = sequence_rows // BLK
    step_rows = SUB_BLOCKS * BLK
    return pl.pallas_call(
        attend_kernel,
        out_shape=jax.ShapeDtypeStruct((sequence_rows, HD), jnp.bfloat16),
        grid_spec=pltpu.PrefetchScalarGridSpec(
            num_scalar_prefetch=2,
            grid=(block_total // SUB_BLOCKS,),
            in_specs=[
                pl.BlockSpec((step_rows, HD), lambda i, lists, counts: (i, 0)),
                pl.BlockSpec((HD, sequence_rows), lambda i, lists, counts: (0, 0)),
                pl.BlockSpec((sequence_rows, HD), lambda i, lists, counts: (0, 1)),
            ],
            out_specs=pl.BlockSpec((step_rows, HD), lambda i, lists, counts: (i, 0)),
        ),
        compiler_params=pltpu.CompilerParams(dimension_semantics=("arbitrary",)),
    )(lists_flat, counts, head_queries, key_t, kv_rows)


ALL_AXES = ("zh", "core", "x", "y", "zl")
CTX_AXES = ("x", "y", "zl")
DP_AXES = ("zh", "core")


def linear_index(zh, core, x, y, zl):
    return (((zh * 2 + core) * 4 + x) * 4 + y) * 2 + zl


def cross_half_pairs(flip_core):
    pairs = []
    for zh in range(2):
        for core in range(2):
            for x in range(4):
                for y in range(4):
                    for zl in range(2):
                        target_core = 1 - core if flip_core else core
                        pairs.append(
                            (linear_index(zh, core, x, y, zl), linear_index(1 - zh, target_core, x, y, 1 - zl))
                        )
    return pairs


def on_device(hidden, norm_gain, queries, key_weight, value_weight, block_lists, block_counts):
    head_queries = lax.all_to_all(queries[0], CTX_AXES, split_axis=1, concat_axis=0, tiled=True)
    upcast = hidden[0].astype(jnp.float32)
    mean_square = jnp.mean(upcast * upcast, axis=-1, keepdims=True)
    normed = (upcast * lax.rsqrt(mean_square + 1e-05) * norm_gain.astype(jnp.float32)).astype(
        jnp.bfloat16
    )
    local_rows, features = normed.shape
    local_weight = (key_weight, value_weight)
    weight_rows = key_weight.shape[0]
    half_features = 2 * weight_rows
    zh = lax.axis_index("zh")
    core = lax.axis_index("core")
    partner_pairs = cross_half_pairs(False)
    sibling = lax.ppermute(local_weight, "core", [(0, 1), (1, 0)])

    def half_sum(rows, offset):
        own = lax.dynamic_slice_in_dim(rows, offset + core * weight_rows, weight_rows, axis=1)
        other = lax.dynamic_slice_in_dim(rows, offset + (1 - core) * weight_rows, weight_rows, axis=1)
        return jnp.concatenate(
            [
                jnp.dot(own, mine, preferred_element_type=jnp.float32)
                + jnp.dot(other, theirs, preferred_element_type=jnp.float32)
                for mine, theirs in zip(local_weight, sibling)
            ],
            axis=1,
        )

    ctx_size = lax.axis_size(CTX_AXES)
    copies_per_head = ctx_size // KVH
    chunk_rows = local_rows // CHUNKS
    kv_chunks = []
    for chunk in range(CHUNKS):
        rows = normed[chunk * chunk_rows : (chunk + 1) * chunk_rows]
        far_features = lax.dynamic_slice_in_dim(rows, (1 - zh) * half_features, half_features, axis=1)
        partner_rows = lax.ppermute(far_features, ALL_AXES, partner_pairs)
        if chunk == 0:
            head_queries, partner_rows = lax.optimization_barrier((head_queries, partner_rows))
        from_partner = lax.ppermute(half_sum(partner_rows, 0), ALL_AXES, partner_pairs)
        summed = half_sum(rows, zh * half_features) + from_partner
        paired = summed.reshape(chunk_rows, 2, KVH, 1, HD).astype(jnp.bfloat16)
        widened = jnp.broadcast_to(paired, (chunk_rows, 2, KVH, copies_per_head, HD))
        widened = widened.reshape(chunk_rows, 2, ctx_size, HD)
        kv_chunks.append(lax.all_to_all(widened, CTX_AXES, split_axis=2, concat_axis=0, tiled=True))
    head_pair = jnp.concatenate(kv_chunks, axis=0)
    sequence_rows = head_queries.shape[0]
    kv_rows = head_pair.reshape(sequence_rows, 2 * HD)
    key_t = kv_rows[:, :HD].T
    lists = block_lists[0, 0]
    lists_flat = ((lists % CHUNKS) * ctx_size + lists // CHUNKS).reshape(-1)
    counts = block_counts[0, 0]
    attended_head = attend(lists_flat, counts, head_queries, key_t, kv_rows)
    restored = lax.all_to_all(attended_head, CTX_AXES, split_axis=0, concat_axis=1, tiled=True)
    return restored[None]


def solution(mesh):
    fine = jax.sharding.Mesh(mesh.devices.reshape(2, 2, 4, 4, 2), ALL_AXES)
    return jax.shard_map(
        on_device,
        mesh=fine,
        in_specs=(
            P(DP_AXES, CTX_AXES, None),
            P(),
            P(DP_AXES, CTX_AXES, None),
            P(DP_AXES, None),
            P(DP_AXES, None),
            P(DP_AXES, CTX_AXES, None, None),
            P(DP_AXES, CTX_AXES, None),
        ),
        out_specs=P(DP_AXES, CTX_AXES, None),
        check_vma=False,
    )
```

```python
import jax
import jax.numpy as jnp
from jax import lax
from jax.experimental import pallas as pl
from jax.experimental.pallas import tpu as pltpu
from jax.sharding import PartitionSpec as P

KVH = 4
HD = 128
BLK = 128
MAXB = 12


SUB_BLOCKS = 8
CHUNKS = 2


def attend_kernel(lists_ref, counts_ref, q_ref, kt_ref, v_ref, o_ref):
    step = pl.program_id(0)
    score_scale = HD ** (-0.5)
    rows = lax.broadcasted_iota(jnp.int32, (BLK, BLK), 0)
    cols = lax.broadcasted_iota(jnp.int32, (BLK, BLK), 1)

    def one_block(sub, carry):
        block = step * SUB_BLOCKS + sub
        first_row = pl.multiple_of(sub * BLK, BLK)
        query = q_ref[pl.ds(first_row, BLK), :]
        count = counts_ref[block]
        masked = []
        for slot in range(MAXB):
            start = pl.multiple_of(lists_ref[block * MAXB + slot] * BLK, BLK)
            key_tile = kt_ref[:, pl.ds(start, BLK)]
            scores = jnp.dot(query, key_tile, preferred_element_type=jnp.float32) * score_scale
            allowed = slot < count
            if slot == 0:
                allowed = jnp.logical_and(allowed, cols <= rows)
            masked.append(jnp.where(allowed, scores, -jnp.inf))
        peak = masked[0]
        for scores in masked[1:]:
            peak = jnp.maximum(peak, scores)
        row_peak = jnp.max(peak, axis=1, keepdims=True)
        column_sums = jnp.zeros((BLK, BLK), jnp.float32)
        weighted = jnp.zeros((BLK, HD), jnp.float32)
        for slot in range(MAXB):
            start = pl.multiple_of(lists_ref[block * MAXB + slot] * BLK, BLK)
            value_tile = v_ref[pl.ds(start, BLK), :]
            exponent = jnp.exp(masked[slot] - row_peak)
            column_sums = column_sums + exponent
            weighted = weighted + jnp.dot(
                exponent.astype(jnp.bfloat16), value_tile, preferred_element_type=jnp.float32
            )
        denominator = jnp.sum(column_sums, axis=1, keepdims=True)
        o_ref[pl.ds(first_row, BLK), :] = (weighted / denominator).astype(o_ref.dtype)
        return carry

    lax.fori_loop(0, SUB_BLOCKS, one_block, 0, unroll=8)


def attend(lists_flat, counts, head_queries, key_t, kv_rows):
    sequence_rows = head_queries.shape[0]
    block_total = sequence_rows // BLK
    step_rows = SUB_BLOCKS * BLK
    return pl.pallas_call(
        attend_kernel,
        out_shape=jax.ShapeDtypeStruct((sequence_rows, HD), jnp.bfloat16),
        grid_spec=pltpu.PrefetchScalarGridSpec(
            num_scalar_prefetch=2,
            grid=(block_total // SUB_BLOCKS,),
            in_specs=[
                pl.BlockSpec((step_rows, HD), lambda i, lists, counts: (i, 0)),
                pl.BlockSpec((HD, sequence_rows), lambda i, lists, counts: (0, 0)),
                pl.BlockSpec((sequence_rows, HD), lambda i, lists, counts: (0, 1)),
            ],
            out_specs=pl.BlockSpec((step_rows, HD), lambda i, lists, counts: (i, 0)),
        ),
        compiler_params=pltpu.CompilerParams(dimension_semantics=("arbitrary",)),
    )(lists_flat, counts, head_queries, key_t, kv_rows)


ALL_AXES = ("zh", "core", "x", "y", "zl")
CTX_AXES = ("x", "y", "zl")
DP_AXES = ("zh", "core")


def linear_index(zh, core, x, y, zl):
    return (((zh * 2 + core) * 4 + x) * 4 + y) * 2 + zl


def cross_half_pairs(flip_core):
    pairs = []
    for zh in range(2):
        for core in range(2):
            for x in range(4):
                for y in range(4):
                    for zl in range(2):
                        target_core = 1 - core if flip_core else core
                        pairs.append(
                            (linear_index(zh, core, x, y, zl), linear_index(1 - zh, target_core, x, y, 1 - zl))
                        )
    return pairs


def on_device(hidden, norm_gain, queries, key_weight, value_weight, block_lists, block_counts):
    upcast = hidden[0].astype(jnp.float32)
    mean_square = jnp.mean(upcast * upcast, axis=-1, keepdims=True)
    normed = (upcast * lax.rsqrt(mean_square + 1e-05) * norm_gain.astype(jnp.float32)).astype(
        jnp.bfloat16
    )
    local_rows, features = normed.shape
    local_weight = jnp.concatenate([key_weight, value_weight], axis=1)
    weight_rows = local_weight.shape[0]
    half_features = 2 * weight_rows
    zh = lax.axis_index("zh")
    core = lax.axis_index("core")
    partner_pairs = cross_half_pairs(False)
    sibling = lax.ppermute(local_weight, "core", [(0, 1), (1, 0)])

    def half_sum(rows, offset):
        own = lax.dynamic_slice_in_dim(rows, offset + core * weight_rows, weight_rows, axis=1)
        other = lax.dynamic_slice_in_dim(rows, offset + (1 - core) * weight_rows, weight_rows, axis=1)
        return jnp.dot(own, local_weight, preferred_element_type=jnp.float32) + jnp.dot(
            other, sibling, preferred_element_type=jnp.float32
        )

    ctx_size = lax.axis_size(CTX_AXES)
    copies_per_head = ctx_size // KVH
    chunk_rows = local_rows // CHUNKS
    kv_chunks = []
    for chunk in range(CHUNKS):
        rows = normed[chunk * chunk_rows : (chunk + 1) * chunk_rows]
        far_features = lax.dynamic_slice_in_dim(rows, (1 - zh) * half_features, half_features, axis=1)
        partner_rows = lax.ppermute(far_features, ALL_AXES, partner_pairs)
        for_partner = half_sum(partner_rows, 0)
        if chunk == 0:
            local_queries, for_partner = lax.optimization_barrier((queries[0], for_partner))
            head_queries = lax.all_to_all(local_queries, CTX_AXES, split_axis=1, concat_axis=0, tiled=True)
        from_partner = lax.ppermute(for_partner, ALL_AXES, partner_pairs)
        summed = half_sum(rows, zh * half_features) + from_partner
        paired = summed.reshape(chunk_rows, 2, KVH, 1, HD).astype(jnp.bfloat16)
        widened = jnp.broadcast_to(paired, (chunk_rows, 2, KVH, copies_per_head, HD))
        widened = widened.reshape(chunk_rows, 2, ctx_size, HD)
        if chunk == 0:
            head_queries, widened = lax.optimization_barrier((head_queries, widened))
        kv_chunks.append(lax.all_to_all(widened, CTX_AXES, split_axis=2, concat_axis=0, tiled=True))
    head_pair = jnp.concatenate(kv_chunks, axis=0)
    sequence_rows = head_queries.shape[0]
    kv_rows = head_pair.reshape(sequence_rows, 2 * HD)
    key_t = kv_rows[:, :HD].T
    lists = block_lists[0, 0]
    lists_flat = ((lists % CHUNKS) * ctx_size + lists // CHUNKS).reshape(-1)
    counts = block_counts[0, 0]
    attended_head = attend(lists_flat, counts, head_queries, key_t, kv_rows)
    restored = lax.all_to_all(attended_head, CTX_AXES, split_axis=0, concat_axis=1, tiled=True)
    return restored[None]


def solution(mesh):
    fine = jax.sharding.Mesh(mesh.devices.reshape(2, 2, 4, 4, 2), ALL_AXES)
    return jax.shard_map(
        on_device,
        mesh=fine,
        in_specs=(
            P(DP_AXES, CTX_AXES, None),
            P(),
            P(DP_AXES, CTX_AXES, None),
            P(DP_AXES, None),
            P(DP_AXES, None),
            P(DP_AXES, CTX_AXES, None, None),
            P(DP_AXES, CTX_AXES, None),
        ),
        out_specs=P(DP_AXES, CTX_AXES, None),
        check_vma=False,
    )
```

```python
import jax
import jax.numpy as jnp
from jax import lax
from jax.experimental import pallas as pl
from jax.experimental.pallas import tpu as pltpu
from jax.sharding import PartitionSpec as P

KVH = 4
HD = 128
BLK = 128
MAXB = 12


SUB_BLOCKS = 16
CHUNKS = 2


def attend_kernel(lists_ref, counts_ref, q_ref, kt_ref, v_ref, o_ref):
    step = pl.program_id(0)
    score_scale = HD ** (-0.5)
    rows = lax.broadcasted_iota(jnp.int32, (BLK, BLK), 0)
    cols = lax.broadcasted_iota(jnp.int32, (BLK, BLK), 1)

    def one_block(sub, carry):
        block = step * SUB_BLOCKS + sub
        first_row = pl.multiple_of(sub * BLK, BLK)
        query = q_ref[pl.ds(first_row, BLK), :]
        count = counts_ref[block]
        masked = []
        for slot in range(MAXB):
            start = pl.multiple_of(lists_ref[block * MAXB + slot] * BLK, BLK)
            key_tile = kt_ref[:, pl.ds(start, BLK)]
            scores = jnp.dot(query, key_tile, preferred_element_type=jnp.float32) * score_scale
            allowed = slot < count
            if slot == 0:
                allowed = jnp.logical_and(allowed, cols <= rows)
            masked.append(jnp.where(allowed, scores, -jnp.inf))
        peak = masked[0]
        for scores in masked[1:]:
            peak = jnp.maximum(peak, scores)
        row_peak = jnp.max(peak, axis=1, keepdims=True)
        column_sums = jnp.zeros((BLK, BLK), jnp.float32)
        weighted = jnp.zeros((BLK, HD), jnp.float32)
        for slot in range(MAXB):
            start = pl.multiple_of(lists_ref[block * MAXB + slot] * BLK, BLK)
            value_tile = v_ref[pl.ds(start, BLK), :]
            exponent = jnp.exp(masked[slot] - row_peak)
            column_sums = column_sums + exponent
            weighted = weighted + jnp.dot(
                exponent.astype(jnp.bfloat16), value_tile, preferred_element_type=jnp.float32
            )
        denominator = jnp.sum(column_sums, axis=1, keepdims=True)
        o_ref[pl.ds(first_row, BLK), :] = (weighted / denominator).astype(o_ref.dtype)
        return carry

    lax.fori_loop(0, SUB_BLOCKS, one_block, 0, unroll=16)


def attend(lists_flat, counts, head_queries, key_t, kv_rows):
    sequence_rows = head_queries.shape[0]
    block_total = sequence_rows // BLK
    step_rows = SUB_BLOCKS * BLK
    return pl.pallas_call(
        attend_kernel,
        out_shape=jax.ShapeDtypeStruct((sequence_rows, HD), jnp.bfloat16),
        grid_spec=pltpu.PrefetchScalarGridSpec(
            num_scalar_prefetch=2,
            grid=(block_total // SUB_BLOCKS,),
            in_specs=[
                pl.BlockSpec((step_rows, HD), lambda i, lists, counts: (i, 0)),
                pl.BlockSpec((HD, sequence_rows), lambda i, lists, counts: (0, 0)),
                pl.BlockSpec((sequence_rows, HD), lambda i, lists, counts: (0, 1)),
            ],
            out_specs=pl.BlockSpec((step_rows, HD), lambda i, lists, counts: (i, 0)),
        ),
        compiler_params=pltpu.CompilerParams(dimension_semantics=("arbitrary",)),
    )(lists_flat, counts, head_queries, key_t, kv_rows)


ALL_AXES = ("zh", "core", "x", "y", "zl")
CTX_AXES = ("x", "y", "zl")
DP_AXES = ("zh", "core")


def linear_index(zh, core, x, y, zl):
    return (((zh * 2 + core) * 4 + x) * 4 + y) * 2 + zl


def cross_half_pairs(flip_core):
    pairs = []
    for zh in range(2):
        for core in range(2):
            for x in range(4):
                for y in range(4):
                    for zl in range(2):
                        target_core = 1 - core if flip_core else core
                        pairs.append(
                            (linear_index(zh, core, x, y, zl), linear_index(1 - zh, target_core, x, y, 1 - zl))
                        )
    return pairs


def on_device(hidden, norm_gain, queries, key_weight, value_weight, block_lists, block_counts):
    head_queries = lax.all_to_all(queries[0], CTX_AXES, split_axis=1, concat_axis=0, tiled=True)
    upcast = hidden[0].astype(jnp.float32)
    mean_square = jnp.mean(upcast * upcast, axis=-1, keepdims=True)
    normed = (upcast * lax.rsqrt(mean_square + 1e-05) * norm_gain.astype(jnp.float32)).astype(
        jnp.bfloat16
    )
    local_rows, features = normed.shape
    local_weight = jnp.concatenate([key_weight, value_weight], axis=1)
    weight_rows = local_weight.shape[0]
    half_features = 2 * weight_rows
    zh = lax.axis_index("zh")
    core = lax.axis_index("core")
    partner_pairs = cross_half_pairs(False)
    sibling = lax.ppermute(local_weight, "core", [(0, 1), (1, 0)])

    def half_sum(rows, offset):
        own = lax.dynamic_slice_in_dim(rows, offset + core * weight_rows, weight_rows, axis=1)
        other = lax.dynamic_slice_in_dim(rows, offset + (1 - core) * weight_rows, weight_rows, axis=1)
        return jnp.dot(own, local_weight, preferred_element_type=jnp.float32) + jnp.dot(
            other, sibling, preferred_element_type=jnp.float32
        )

    ctx_size = lax.axis_size(CTX_AXES)
    copies_per_head = ctx_size // KVH
    chunk_rows = local_rows // CHUNKS
    kv_chunks = []
    for chunk in range(CHUNKS):
        rows = normed[chunk * chunk_rows : (chunk + 1) * chunk_rows]
        far_features = lax.dynamic_slice_in_dim(rows, (1 - zh) * half_features, half_features, axis=1)
        partner_rows = lax.ppermute(far_features, ALL_AXES, partner_pairs)
        if chunk == 0:
            head_queries, partner_rows = lax.optimization_barrier((head_queries, partner_rows))
        from_partner = lax.ppermute(half_sum(partner_rows, 0), ALL_AXES, partner_pairs)
        summed = half_sum(rows, zh * half_features) + from_partner
        paired = summed.reshape(chunk_rows, 2, KVH, 1, HD).astype(jnp.bfloat16)
        widened = jnp.broadcast_to(paired, (chunk_rows, 2, KVH, copies_per_head, HD))
        widened = widened.reshape(chunk_rows, 2, ctx_size, HD)
        kv_chunks.append(lax.all_to_all(widened, CTX_AXES, split_axis=2, concat_axis=0, tiled=True))
    head_pair = jnp.concatenate(kv_chunks, axis=0)
    sequence_rows = head_queries.shape[0]
    kv_rows = head_pair.reshape(sequence_rows, 2 * HD)
    key_t = kv_rows[:, :HD].T
    lists = block_lists[0, 0]
    lists_flat = ((lists % CHUNKS) * ctx_size + lists // CHUNKS).reshape(-1)
    counts = block_counts[0, 0]
    attended_head = attend(lists_flat, counts, head_queries, key_t, kv_rows)
    restored = lax.all_to_all(attended_head, CTX_AXES, split_axis=0, concat_axis=1, tiled=True)
    return restored[None]


def solution(mesh):
    fine = jax.sharding.Mesh(mesh.devices.reshape(2, 2, 4, 4, 2), ALL_AXES)
    return jax.shard_map(
        on_device,
        mesh=fine,
        in_specs=(
            P(DP_AXES, CTX_AXES, None),
            P(),
            P(DP_AXES, CTX_AXES, None),
            P(DP_AXES, None),
            P(DP_AXES, None),
            P(DP_AXES, CTX_AXES, None, None),
            P(DP_AXES, CTX_AXES, None),
        ),
        out_specs=P(DP_AXES, CTX_AXES, None),
        check_vma=False,
    )
```
